32 devices in a mesh: groups: 2 (over y), seq: 8 (over z, x), head: 2 (over core).
Axes of the slice: x: 2, y: 2, z: 4, core: 2. Of those that a mesh axis runs over, the one named last changes fastest.
Arguments:
- query_vectors: bfloat16 [2, 16384, 512], P(None, ('groups', 'seq'), 'head'), parts along dimension 1, may hold values from -8 to 8
- key_vectors: bfloat16 [2, 16384, 512], P(None, ('groups', 'seq'), 'head'), parts along dimension 1, may hold values from -8 to 8
- value_vectors: bfloat16 [2, 16384, 512], P(None, ('groups', 'seq'), 'head'), parts along dimension 1, may hold values from -12 to 12
Outputs:
- attended: bfloat16 [2, 16384, 512], P(None, ('groups', 'seq'), 'head'), parts along dimension 1
The draws below stay inside these ranges and needn't reach their ends.
There are 2 independent parts, one for each index of `groups`. The reference program is written for one: setup_inputs(seed, part) draws one part's arguments, and reference() takes and returns one part's arrays. A program takes and returns all parts, laid end to end along the dimension named above; each array names one. Nothing has to cross between parts.
All inputs are finite; a program needn't handle non-finite values.
Results may differ from the reference program's by a relative error of at most 0.0039.
Values may be sent and summed in bfloat16 or wider, within the bound.
No kernel may reach another device: no remote copies, remote signals or barrier semaphores. Data moves between devices by JAX's collectives and lax.ppermute only.
A program may use at most 64 MiB of HBM per device.

```python
import math
import jax
import jax.numpy as jnp
from jax import lax

DH = 128
STRIDE = 1024
HALF = 4
ROWS = 8
TOKENS = 8192


def build_pair(key):
    extent = (2, TOKENS, HALF, DH)
    queries = 1.4 * jax.random.truncated_normal(jax.random.fold_in(key, 101), -5.5, 5.5, extent)
    keys_drawn = 1.4 * jax.random.truncated_normal(jax.random.fold_in(key, 102), -5.5, 5.5, extent)
    return (queries.reshape(2, TOKENS, HALF * DH), keys_drawn.reshape(2, TOKENS, HALF * DH))


def draw_query_vectors(key, part):
    return build_pair(key)[0].astype(jnp.bfloat16)


def draw_key_vectors(key, part):
    return build_pair(key)[1].astype(jnp.bfloat16)


def levels(stream_key, shape, shards, low, largest):
    loudness, own = 1.0, jax.random.fold_in(stream_key, 6)
    for dim, blocks in shards:
        heights = jnp.exp(jax.random.uniform(jax.random.fold_in(own, dim), (blocks,), jnp.float32, low / len(shards), largest / len(shards)))
        loudness = loudness * jnp.repeat(heights, shape[dim] // blocks).reshape([-1 if axis == dim else 1 for axis in range(len(shape))])
    return loudness


def centred(key, shape, width, reach, split=(), kind=jnp.bfloat16):
    loudness = levels(key, shape, split, -0.22, 0.18) if split else 1.0
    values = jax.random.normal(key, shape, jnp.float32) * width * loudness
    return jnp.minimum(jnp.maximum(values, -reach), reach).astype(kind)


def setup_inputs(seed: int = 0, part: int = 0) -> dict:
    streams_of = jax.random.split(jax.random.key(seed), 4)
    own_keys = jax.random.split(jax.random.fold_in(streams_of[3], part), 4)
    query_vectors = draw_query_vectors(jax.random.fold_in(jax.random.fold_in(streams_of[3], part), 71), part)
    key_vectors = draw_key_vectors(jax.random.fold_in(jax.random.fold_in(streams_of[3], part), 71), part)
    value_vectors = centred(own_keys[2], (2, TOKENS, HALF * DH), 2.0, 12.0, ((1, 8), (2, 2)))
    return {"query_vectors": query_vectors, "key_vectors": key_vectors, "value_vectors": value_vectors}


def reference(query_vectors, key_vectors, value_vectors):
    score_scale = 1.0 / math.sqrt(DH)
    block_size = min(512, TOKENS)
    queries = query_vectors.astype(jnp.float32).reshape(2, TOKENS, HALF, DH)
    keys_all = key_vectors.astype(jnp.float32).reshape(2, TOKENS, HALF, DH)
    values_all = value_vectors.astype(jnp.float32).reshape(2, TOKENS, HALF, DH)
    padding = jnp.zeros((STRIDE, HALF, DH), jnp.float32)
    padded_keys = jnp.concatenate([padding, keys_all[0]], axis=0)
    padded_values = jnp.concatenate([padding, values_all[0]], axis=0)

    def row_step(offset):
        query_block = lax.dynamic_slice_in_dim(queries[0], offset, block_size, 0)
        key_block = lax.dynamic_slice_in_dim(padded_keys, offset, STRIDE + block_size, 0)
        value_block = lax.dynamic_slice_in_dim(padded_values, offset, STRIDE + block_size, 0)
        scores = jnp.einsum('qhd,khd->hqk', query_block, key_block) * score_scale
        query_pos = jnp.arange(block_size, dtype=jnp.int32)[:, None]
        key_pos = jnp.arange(STRIDE + block_size, dtype=jnp.int32)[None, :]
        allowed = (key_pos > query_pos) & (key_pos <= STRIDE + query_pos) & (offset + key_pos >= STRIDE)
        scores = jnp.where(allowed[None], scores, -jnp.inf)
        maxima = lax.optimization_barrier(jnp.max(scores, axis=-1, keepdims=True))
        expo = jnp.exp(scores - maxima)
        weights = (expo / lax.optimization_barrier(jnp.sum(expo, axis=-1, keepdims=True))).astype(jnp.bfloat16)
        return jnp.einsum('hqk,khd->qhd', weights.astype(jnp.float32), value_block).astype(jnp.bfloat16)
    starts = jnp.arange(TOKENS // block_size, dtype=jnp.int32) * block_size
    row_out = lax.map(row_step, starts).reshape(TOKENS, HALF * DH)
    column_block = min(128, STRIDE)

    def to_blocks(array):
        grid = array.reshape(ROWS, STRIDE // column_block, column_block, HALF, DH)
        return jnp.moveaxis(grid, 1, 0)

    def column_step(pieces):
        query_cols, key_cols, value_cols = pieces
        scores = jnp.einsum('rchd,schd->chrs', query_cols, key_cols) * score_scale
        row_pos = jnp.arange(ROWS, dtype=jnp.int32)[:, None]
        other_pos = jnp.arange(ROWS, dtype=jnp.int32)[None, :]
        allowed = other_pos <= row_pos
        scores = jnp.where(allowed[None, None], scores, -jnp.inf)
        maxima = lax.optimization_barrier(jnp.max(scores, axis=-1, keepdims=True))
        expo = jnp.exp(scores - maxima)
        weights = (expo / lax.optimization_barrier(jnp.sum(expo, axis=-1, keepdims=True))).astype(jnp.bfloat16)
        return jnp.einsum('chrs,schd->rchd', weights.astype(jnp.float32), value_cols).astype(jnp.bfloat16)
    column_parts = lax.map(column_step, (to_blocks(queries[1]), to_blocks(keys_all[1]), to_blocks(values_all[1])))
    column_out = jnp.moveaxis(column_parts, 0, 1).reshape(TOKENS, HALF * DH)
    return jnp.stack([row_out, column_out])
```

```python
import functools
import math

import jax
import jax.numpy as jnp
from jax import lax
from jax.experimental import pallas as pl
from jax.experimental.pallas import tpu as pltpu
from jax.sharding import PartitionSpec as P

DH = 128
STRIDE = 1024
QUERY_TILE = 256


def shifted(block, axis, distance):
    devices = range(lax.axis_size(axis))
    route = [(i - distance, i) for i in devices if i - distance in devices]
    return lax.ppermute(block, axis, route)


def attend_columns(query_cols, key_cols, value_cols):
    score_scale = 1.0 / math.sqrt(DH)
    scores = (
        jnp.einsum("rchd,schd->chrs", query_cols, key_cols, preferred_element_type=jnp.float32)
        * score_scale
    )
    count = query_cols.shape[0]
    row_pos = jnp.arange(count, dtype=jnp.int32)[:, None]
    other_pos = jnp.arange(count, dtype=jnp.int32)[None, :]
    allowed = other_pos <= row_pos
    scores = jnp.where(allowed[None, None], scores, -jnp.inf)
    maxima = jnp.max(scores, axis=-1, keepdims=True)
    expo = jnp.exp(scores - maxima)
    weights = (expo / jnp.sum(expo, axis=-1, keepdims=True)).astype(jnp.bfloat16)
    return jnp.einsum(
        "chrs,schd->rchd", weights, value_cols, preferred_element_type=jnp.float32
    ).astype(jnp.bfloat16)


def row_kernel(flag_ref, q_ref, kp_ref, kc_ref, vp_ref, vc_ref, o_ref):
    tile = pl.program_id(1)
    score_scale = 1.0 / math.sqrt(DH)
    dims = (((1,), (1,)), ((), ()))
    q = q_ref[...]
    prev_scores = lax.dot_general(q, kp_ref[...], dims, preferred_element_type=jnp.float32) * score_scale
    cur_scores = lax.dot_general(q, kc_ref[...], dims, preferred_element_type=jnp.float32) * score_scale
    tq = q.shape[0]
    query_pos = tile * tq + lax.broadcasted_iota(jnp.int32, (tq, STRIDE), 0)
    key_pos = lax.broadcasted_iota(jnp.int32, (tq, STRIDE), 1)
    has_prev = flag_ref[0] > 0
    prev_scores = jnp.where((key_pos > query_pos) & has_prev, prev_scores, -jnp.inf)
    cur_scores = jnp.where(key_pos <= query_pos, cur_scores, -jnp.inf)
    maxima = jnp.maximum(
        jnp.max(prev_scores, axis=1, keepdims=True), jnp.max(cur_scores, axis=1, keepdims=True)
    )
    prev_expo = jnp.exp(prev_scores - maxima)
    cur_expo = jnp.exp(cur_scores - maxima)
    total = jnp.sum(prev_expo, axis=1, keepdims=True) + jnp.sum(cur_expo, axis=1, keepdims=True)
    prev_w = (prev_expo / total).astype(jnp.bfloat16)
    cur_w = (cur_expo / total).astype(jnp.bfloat16)
    out = jnp.dot(prev_w, vp_ref[...], preferred_element_type=jnp.float32)
    out = out + jnp.dot(cur_w, vc_ref[...], preferred_element_type=jnp.float32)
    o_ref[...] = out.astype(o_ref.dtype)


def attend_rows(has_prev, queries, prev_keys, keys, prev_values, values):
    tokens, width = queries.shape
    heads = width // DH
    tiles = tokens // QUERY_TILE
    q_spec = pl.BlockSpec((QUERY_TILE, DH), lambda h, t, flag: (t, h))
    kv_spec = pl.BlockSpec((STRIDE, DH), lambda h, t, flag: (0, h))
    scores = heads * tokens * 2 * STRIDE
    return pl.pallas_call(
        row_kernel,
        out_shape=jax.ShapeDtypeStruct((tokens, width), jnp.bfloat16),
        grid_spec=pltpu.PrefetchScalarGridSpec(
            num_scalar_prefetch=1,
            grid=(heads, tiles),
            in_specs=[q_spec, kv_spec, kv_spec, kv_spec, kv_spec],
            out_specs=q_spec,
        ),
        cost_estimate=pl.CostEstimate(
            flops=4 * scores * DH, transcendentals=scores, bytes_accessed=6 * tokens * width * 2
        ),
    )(has_prev, queries, prev_keys, keys, prev_values, values)


def local(query_vectors, key_vectors, value_vectors):
    local_tokens = query_vectors.shape[1]
    feature_width = query_vectors.shape[2]
    heads_here = feature_width // DH
    rows_here = local_tokens // STRIDE
    assert rows_here == 1
    seq_index = lax.axis_index("seq")
    prev_keys, prev_values = shifted(
        (key_vectors[0, local_tokens - STRIDE :], value_vectors[0, local_tokens - STRIDE :]),
        "seq",
        1,
    )
    stacked = jnp.stack([query_vectors[1], key_vectors[1], value_vectors[1]]).reshape(
        3, rows_here, STRIDE, heads_here, DH
    )
    moved = lax.all_to_all(stacked, "seq", split_axis=2, concat_axis=1, tiled=True)
    result = attend_columns(moved[0], moved[1], moved[2])
    context = lax.all_to_all(result, "seq", split_axis=0, concat_axis=1, tiled=True)
    column_out = context.reshape(local_tokens, feature_width)
    has_prev = (seq_index > 0).astype(jnp.int32).reshape(1)
    row_out = attend_rows(
        has_prev, query_vectors[0], prev_keys, key_vectors[0], prev_values, value_vectors[0]
    )
    return jnp.stack([row_out, column_out])


def solution(mesh):
    return jax.shard_map(
        local,
        mesh=mesh,
        in_specs=(
            P(None, ("groups", "seq"), "head"),
            P(None, ("groups", "seq"), "head"),
            P(None, ("groups", "seq"), "head"),
        ),
        out_specs=P(None, ("groups", "seq"), "head"),
        check_vma=False,
    )
```

```python
import functools
import math

import jax
import jax.numpy as jnp
from jax import lax
from jax.experimental import pallas as pl
from jax.experimental.pallas import tpu as pltpu
from jax.sharding import PartitionSpec as P

DH = 128
STRIDE = 1024
QUERY_TILE = 256


def shifted(block, axis, distance):
    devices = range(lax.axis_size(axis))
    route = [(i - distance, i) for i in devices if i - distance in devices]
    return lax.ppermute(block, axis, route)


def attend_columns(query_cols, key_cols, value_cols):
    score_scale = 1.0 / math.sqrt(DH)
    scores = (
        jnp.einsum("rchd,schd->chrs", query_cols, key_cols, preferred_element_type=jnp.float32)
        * score_scale
    )
    count = query_cols.shape[0]
    row_pos = jnp.arange(count, dtype=jnp.int32)[:, None]
    other_pos = jnp.arange(count, dtype=jnp.int32)[None, :]
    allowed = other_pos <= row_pos
    scores = jnp.where(allowed[None, None], scores, -jnp.inf)
    maxima = jnp.max(scores, axis=-1, keepdims=True)
    expo = jnp.exp(scores - maxima)
    weights = (expo / jnp.sum(expo, axis=-1, keepdims=True)).astype(jnp.bfloat16)
    return jnp.einsum(
        "chrs,schd->rchd", weights, value_cols, preferred_element_type=jnp.float32
    ).astype(jnp.bfloat16)


def row_kernel(flag_ref, q_ref, kp_ref, kc_ref, vp_ref, vc_ref, o_ref):
    score_scale = 1.0 / math.sqrt(DH)
    dims = (((1,), (1,)), ((), ()))
    has_prev = flag_ref[0] > 0
    tq = QUERY_TILE
    for tile in range(STRIDE // tq):
        low, high = tile * tq, (tile + 1) * tq
        q = q_ref[low:high, :]
        prev_scores = (
            lax.dot_general(q, kp_ref[low:, :], dims, preferred_element_type=jnp.float32)
            * score_scale
        )
        cur_scores = (
            lax.dot_general(q, kc_ref[:high, :], dims, preferred_element_type=jnp.float32)
            * score_scale
        )
        prev_shape = (tq, STRIDE - low)
        prev_ok = lax.broadcasted_iota(jnp.int32, prev_shape, 1) > lax.broadcasted_iota(
            jnp.int32, prev_shape, 0
        )
        cur_shape = (tq, high)
        cur_ok = lax.broadcasted_iota(jnp.int32, cur_shape, 1) <= lax.broadcasted_iota(
            jnp.int32, cur_shape, 0
        ) + low
        prev_scores = jnp.where(prev_ok & has_prev, prev_scores, -jnp.inf)
        cur_scores = jnp.where(cur_ok, cur_scores, -jnp.inf)
        maxima = jnp.maximum(
            jnp.max(prev_scores, axis=1, keepdims=True), jnp.max(cur_scores, axis=1, keepdims=True)
        )
        prev_expo = jnp.exp(prev_scores - maxima)
        cur_expo = jnp.exp(cur_scores - maxima)
        total = jnp.sum(prev_expo, axis=1, keepdims=True) + jnp.sum(cur_expo, axis=1, keepdims=True)
        inverse = 1.0 / total
        prev_w = (prev_expo * inverse).astype(jnp.bfloat16)
        cur_w = (cur_expo * inverse).astype(jnp.bfloat16)
        out = jnp.dot(prev_w, vp_ref[low:, :], preferred_element_type=jnp.float32)
        out = out + jnp.dot(cur_w, vc_ref[:high, :], preferred_element_type=jnp.float32)
        o_ref[low:high, :] = out.astype(o_ref.dtype)


def attend_rows(has_prev, queries, prev_keys, keys, prev_values, values):
    tokens, width = queries.shape
    heads = width // DH
    spec = pl.BlockSpec((STRIDE, DH), lambda h, flag: (0, h))
    scores = heads * tokens * (STRIDE + QUERY_TILE)
    return pl.pallas_call(
        row_kernel,
        out_shape=jax.ShapeDtypeStruct((tokens, width), jnp.bfloat16),
        grid_spec=pltpu.PrefetchScalarGridSpec(
            num_scalar_prefetch=1,
            grid=(heads,),
            in_specs=[spec] * 5,
            out_specs=spec,
        ),
        cost_estimate=pl.CostEstimate(
            flops=4 * scores * DH, transcendentals=scores, bytes_accessed=6 * tokens * width * 2
        ),
    )(has_prev, queries, prev_keys, keys, prev_values, values)


def local(query_vectors, key_vectors, value_vectors):
    local_tokens = query_vectors.shape[1]
    feature_width = query_vectors.shape[2]
    heads_here = feature_width // DH
    assert local_tokens == STRIDE
    blocks = lax.axis_size("seq")
    width = STRIDE // blocks
    seq_index = lax.axis_index("seq")
    prev_keys, prev_values = shifted((key_vectors[0], value_vectors[0]), "seq", 1)
    stacked = jnp.stack(
        [
            query_vectors[1].reshape(blocks, width, feature_width),
            key_vectors[1].reshape(blocks, width, feature_width),
            value_vectors[1].reshape(blocks, width, feature_width),
        ],
        axis=1,
    )
    moved = lax.all_to_all(stacked, "seq", split_axis=0, concat_axis=0, tiled=True)
    moved, prev_keys, prev_values = lax.optimization_barrier((moved, prev_keys, prev_values))
    grid = moved.reshape(blocks, 3, width, heads_here, DH)
    result = attend_columns(grid[:, 0], grid[:, 1], grid[:, 2])
    context = lax.all_to_all(
        result.reshape(blocks, width, feature_width), "seq", split_axis=0, concat_axis=0, tiled=True
    )
    column_out = context.reshape(local_tokens, feature_width)
    has_prev = (seq_index > 0).astype(jnp.int32).reshape(1)
    row_out = attend_rows(
        has_prev, query_vectors[0], prev_keys, key_vectors[0], prev_values, value_vectors[0]
    )
    return jnp.stack([row_out, column_out])


def solution(mesh):
    return jax.shard_map(
        local,
        mesh=mesh,
        in_specs=(
            P(None, ("groups", "seq"), "head"),
            P(None, ("groups", "seq"), "head"),
            P(None, ("groups", "seq"), "head"),
        ),
        out_specs=P(None, ("groups", "seq"), "head"),
        check_vma=False,
    )
```

```python
import functools
import math

import jax
import jax.numpy as jnp
from jax import lax
from jax.experimental import pallas as pl
from jax.experimental.pallas import tpu as pltpu
from jax.sharding import PartitionSpec as P

DH = 128
STRIDE = 1024
QUERY_TILE = 256


def shifted(block, axis, distance):
    devices = range(lax.axis_size(axis))
    route = [(i - distance, i) for i in devices if i - distance in devices]
    return lax.ppermute(block, axis, route)


def attend_columns(query_cols, key_cols, value_cols):
    score_scale = 1.0 / math.sqrt(DH)
    scores = (
        jnp.einsum("rchd,schd->chrs", query_cols, key_cols, preferred_element_type=jnp.float32)
        * score_scale
    )
    count = query_cols.shape[0]
    row_pos = jnp.arange(count, dtype=jnp.int32)[:, None]
    other_pos = jnp.arange(count, dtype=jnp.int32)[None, :]
    allowed = other_pos <= row_pos
    scores = jnp.where(allowed[None, None], scores, -jnp.inf)
    maxima = jnp.max(scores, axis=-1, keepdims=True)
    expo = jnp.exp(scores - maxima)
    weights = (expo / jnp.sum(expo, axis=-1, keepdims=True)).astype(jnp.bfloat16)
    return jnp.einsum(
        "chrs,schd->rchd", weights, value_cols, preferred_element_type=jnp.float32
    ).astype(jnp.bfloat16)


def row_kernel(flag_ref, q_ref, kp_ref, kc_ref, vp_ref, vc_ref, o_ref):
    score_scale = 1.0 / math.sqrt(DH)
    dims = (((1,), (1,)), ((), ()))
    has_prev = flag_ref[0] > 0
    tq = QUERY_TILE
    for tile in range(STRIDE // tq):
        low, high = tile * tq, (tile + 1) * tq
        q = q_ref[low:high, :]
        prev_scores = (
            lax.dot_general(q, kp_ref[low:, :], dims, preferred_element_type=jnp.float32)
            * score_scale
        )
        cur_scores = (
            lax.dot_general(q, kc_ref[:high, :], dims, preferred_element_type=jnp.float32)
            * score_scale
        )
        prev_shape = (tq, STRIDE - low)
        prev_ok = lax.broadcasted_iota(jnp.int32, prev_shape, 1) > lax.broadcasted_iota(
            jnp.int32, prev_shape, 0
        )
        cur_shape = (tq, high)
        cur_ok = lax.broadcasted_iota(jnp.int32, cur_shape, 1) <= lax.broadcasted_iota(
            jnp.int32, cur_shape, 0
        ) + low
        prev_scores = jnp.where(prev_ok & has_prev, prev_scores, -jnp.inf)
        cur_scores = jnp.where(cur_ok, cur_scores, -jnp.inf)
        maxima = jnp.maximum(
            jnp.max(prev_scores, axis=1, keepdims=True), jnp.max(cur_scores, axis=1, keepdims=True)
        )
        prev_expo = jnp.exp(prev_scores - maxima)
        cur_expo = jnp.exp(cur_scores - maxima)
        total = jnp.sum(prev_expo, axis=1, keepdims=True) + jnp.sum(cur_expo, axis=1, keepdims=True)
        inverse = 1.0 / total
        prev_w = (prev_expo * inverse).astype(jnp.bfloat16)
        cur_w = (cur_expo * inverse).astype(jnp.bfloat16)
        out = jnp.dot(prev_w, vp_ref[low:, :], preferred_element_type=jnp.float32)
        out = out + jnp.dot(cur_w, vc_ref[:high, :], preferred_element_type=jnp.float32)
        o_ref[low:high, :] = out.astype(o_ref.dtype)


def attend_rows(has_prev, queries, prev_pair, keys, values):
    tokens, width = queries.shape
    heads = width // DH
    spec = pl.BlockSpec((STRIDE, DH), lambda h, flag: (0, h))
    prev_key_spec = pl.BlockSpec((None, STRIDE, DH), lambda h, flag: (0, 0, h))
    prev_value_spec = pl.BlockSpec((None, STRIDE, DH), lambda h, flag: (1, 0, h))
    scores = heads * tokens * (STRIDE + QUERY_TILE)
    return pl.pallas_call(
        row_kernel,
        out_shape=jax.ShapeDtypeStruct((2, tokens, width), jnp.bfloat16),
        grid_spec=pltpu.PrefetchScalarGridSpec(
            num_scalar_prefetch=1,
            grid=(heads,),
            in_specs=[spec, prev_key_spec, spec, prev_value_spec, spec],
            out_specs=prev_key_spec,
        ),
        cost_estimate=pl.CostEstimate(
            flops=4 * scores * DH, transcendentals=scores, bytes_accessed=6 * tokens * width * 2
        ),
    )(has_prev, queries, prev_pair, keys, prev_pair, values)


def local(query_vectors, key_vectors, value_vectors):
    local_tokens = query_vectors.shape[1]
    feature_width = query_vectors.shape[2]
    heads_here = feature_width // DH
    assert local_tokens == STRIDE
    blocks = lax.axis_size("seq")
    width = STRIDE // blocks
    seq_index = lax.axis_index("seq")
    prev_pair = shifted(jnp.stack([key_vectors[0], value_vectors[0]]), "seq", 1)
    stacked = jnp.stack(
        [
            query_vectors[1].reshape(blocks, width, feature_width),
            key_vectors[1].reshape(blocks, width, feature_width),
            value_vectors[1].reshape(blocks, width, feature_width),
        ],
        axis=1,
    )
    moved = lax.all_to_all(stacked, "seq", split_axis=0, concat_axis=0, tiled=True)
    moved, prev_pair = lax.optimization_barrier((moved, prev_pair))
    grid = moved.reshape(blocks, 3, width, heads_here, DH)
    result = attend_columns(grid[:, 0], grid[:, 1], grid[:, 2])
    context = lax.all_to_all(
        result.reshape(blocks, width, feature_width), "seq", split_axis=0, concat_axis=0, tiled=True
    )
    column_out = context.reshape(local_tokens, feature_width)
    has_prev = (seq_index > 0).astype(jnp.int32).reshape(1)
    both = attend_rows(has_prev, query_vectors[0], prev_pair, key_vectors[0], value_vectors[0])
    return both.at[1].set(column_out)


def solution(mesh):
    return jax.shard_map(
        local,
        mesh=mesh,
        in_specs=(
            P(None, ("groups", "seq"), "head"),
            P(None, ("groups", "seq"), "head"),
            P(None, ("groups", "seq"), "head"),
        ),
        out_specs=P(None, ("groups", "seq"), "head"),
        check_vma=False,
    )
```

```python
import functools
import math

import jax
import jax.numpy as jnp
from jax import lax
from jax.experimental import pallas as pl
from jax.experimental.pallas import tpu as pltpu
from jax.sharding import PartitionSpec as P

DH = 128
STRIDE = 1024
QUERY_TILE = 256


def shifted(block, axis, distance):
    devices = range(lax.axis_size(axis))
    route = [(i - distance, i) for i in devices if i - distance in devices]
    return lax.ppermute(block, axis, route)


def attend_columns(query_cols, key_cols, value_cols):
    score_scale = 1.0 / math.sqrt(DH)
    scores = (
        jnp.einsum("rchd,schd->chrs", query_cols, key_cols, preferred_element_type=jnp.float32)
        * score_scale
    )
    count = query_cols.shape[0]
    row_pos = jnp.arange(count, dtype=jnp.int32)[:, None]
    other_pos = jnp.arange(count, dtype=jnp.int32)[None, :]
    allowed = other_pos <= row_pos
    scores = jnp.where(allowed[None, None], scores, -jnp.inf)
    maxima = jnp.max(scores, axis=-1, keepdims=True)
    expo = jnp.exp(scores - maxima)
    weights = (expo / jnp.sum(expo, axis=-1, keepdims=True)).astype(jnp.bfloat16)
    return jnp.einsum(
        "chrs,schd->rchd", weights, value_cols, preferred_element_type=jnp.float32
    ).astype(jnp.bfloat16)


def row_kernel(flag_ref, q_ref, kp_ref, kc_ref, vp_ref, vc_ref, o_ref):
    score_scale = 1.0 / math.sqrt(DH)
    dims = (((1,), (1,)), ((), ()))
    has_prev = flag_ref[0] > 0
    tq = QUERY_TILE
    for tile in range(STRIDE // tq):
        low, high = tile * tq, (tile + 1) * tq
        q = q_ref[low:high, :]
        prev_scores = (
            lax.dot_general(q, kp_ref[low:, :], dims, preferred_element_type=jnp.float32)
            * score_scale
        )
        cur_scores = (
            lax.dot_general(q, kc_ref[:high, :], dims, preferred_element_type=jnp.float32)
            * score_scale
        )
        prev_shape = (tq, STRIDE - low)
        prev_ok = lax.broadcasted_iota(jnp.int32, prev_shape, 1) > lax.broadcasted_iota(
            jnp.int32, prev_shape, 0
        )
        cur_shape = (tq, high)
        cur_ok = lax.broadcasted_iota(jnp.int32, cur_shape, 1) <= lax.broadcasted_iota(
            jnp.int32, cur_shape, 0
        ) + low
        prev_scores = jnp.where(prev_ok & has_prev, prev_scores, -jnp.inf)
        cur_scores = jnp.where(cur_ok, cur_scores, -jnp.inf)
        maxima = jnp.maximum(
            jnp.max(prev_scores, axis=1, keepdims=True), jnp.max(cur_scores, axis=1, keepdims=True)
        )
        prev_expo = jnp.exp(prev_scores - maxima)
        cur_expo = jnp.exp(cur_scores - maxima)
        total = jnp.sum(prev_expo, axis=1, keepdims=True) + jnp.sum(cur_expo, axis=1, keepdims=True)
        inverse = 1.0 / total
        prev_w = (prev_expo * inverse).astype(jnp.bfloat16)
        cur_w = (cur_expo * inverse).astype(jnp.bfloat16)
        out = jnp.dot(prev_w, vp_ref[low:, :], preferred_element_type=jnp.float32)
        out = out + jnp.dot(cur_w, vc_ref[:high, :], preferred_element_type=jnp.float32)
        o_ref[low:high, :] = out.astype(o_ref.dtype)


def attend_rows(has_prev, queries, prev_pair, keys, values):
    tokens, width = queries.shape
    heads = width // DH
    spec = pl.BlockSpec((STRIDE, DH), lambda h, flag: (0, h))
    prev_key_spec = pl.BlockSpec((None, STRIDE, DH), lambda h, flag: (0, 0, h))
    prev_value_spec = pl.BlockSpec((None, STRIDE, DH), lambda h, flag: (1, 0, h))
    scores = heads * tokens * (STRIDE + QUERY_TILE)
    return pl.pallas_call(
        row_kernel,
        out_shape=jax.ShapeDtypeStruct((2, tokens, width), jnp.bfloat16),
        grid_spec=pltpu.PrefetchScalarGridSpec(
            num_scalar_prefetch=1,
            grid=(heads,),
            in_specs=[spec, prev_key_spec, spec, prev_value_spec, spec],
            out_specs=prev_key_spec,
        ),
        cost_estimate=pl.CostEstimate(
            flops=4 * scores * DH, transcendentals=scores, bytes_accessed=6 * tokens * width * 2
        ),
    )(has_prev, queries, prev_pair, keys, prev_pair, values)


def local(query_vectors, key_vectors, value_vectors):
    local_tokens = query_vectors.shape[1]
    feature_width = query_vectors.shape[2]
    heads_here = feature_width // DH
    assert local_tokens == STRIDE
    blocks = lax.axis_size("seq")
    width = STRIDE // blocks
    seq_index = lax.axis_index("seq")
    prev_pair = shifted(jnp.stack([key_vectors[0], value_vectors[0]]), "seq", 1)
    stacked = jnp.stack(
        [
            query_vectors[1].reshape(blocks, width, feature_width),
            key_vectors[1].reshape(blocks, width, feature_width),
            value_vectors[1].reshape(blocks, width, feature_width),
        ],
        axis=1,
    )
    moved = lax.all_to_all(stacked, "seq", split_axis=0, concat_axis=0, tiled=True)
    _, prev_pair = lax.optimization_barrier((moved, prev_pair))
    grid = moved.reshape(blocks, 3, width, heads_here, DH)
    result = attend_columns(grid[:, 0], grid[:, 1], grid[:, 2])
    context = lax.all_to_all(
        result.reshape(blocks, width, feature_width), "seq", split_axis=0, concat_axis=0, tiled=True
    )
    column_out = context.reshape(local_tokens, feature_width)
    has_prev = (seq_index > 0).astype(jnp.int32).reshape(1)
    both = attend_rows(has_prev, query_vectors[0], prev_pair, key_vectors[0], value_vectors[0])
    return both.at[1].set(column_out)


def solution(mesh):
    return jax.shard_map(
        local,
        mesh=mesh,
        in_specs=(
            P(None, ("groups", "seq"), "head"),
            P(None, ("groups", "seq"), "head"),
            P(None, ("groups", "seq"), "head"),
        ),
        out_specs=P(None, ("groups", "seq"), "head"),
        check_vma=False,
    )
```

```python
import functools
import math

import jax
import jax.numpy as jnp
from jax import lax
from jax.experimental import pallas as pl
from jax.experimental.pallas import tpu as pltpu
from jax.sharding import PartitionSpec as P

DH = 128
STRIDE = 1024
QUERY_TILE = 256


def shifted(block, axis, distance):
    devices = range(lax.axis_size(axis))
    route = [(i - distance, i) for i in devices if i - distance in devices]
    return lax.ppermute(block, axis, route)


def attend_columns(query_cols, key_cols, value_cols):
    score_scale = 1.0 / math.sqrt(DH)
    scores = (
        jnp.einsum("rchd,schd->chrs", query_cols, key_cols, preferred_element_type=jnp.float32)
        * score_scale
    )
    count = query_cols.shape[0]
    row_pos = jnp.arange(count, dtype=jnp.int32)[:, None]
    other_pos = jnp.arange(count, dtype=jnp.int32)[None, :]
    allowed = other_pos <= row_pos
    scores = jnp.where(allowed[None, None], scores, -jnp.inf)
    maxima = jnp.max(scores, axis=-1, keepdims=True)
    expo = jnp.exp(scores - maxima)
    weights = (expo / jnp.sum(expo, axis=-1, keepdims=True)).astype(jnp.bfloat16)
    return jnp.einsum(
        "chrs,schd->rchd", weights, value_cols, preferred_element_type=jnp.float32
    ).astype(jnp.bfloat16)


def row_tiles(with_prev, q_ref, kp_ref, kc_ref, vp_ref, vc_ref, o_ref):
    score_scale = 1.0 / math.sqrt(DH)
    dims = (((1,), (1,)), ((), ()))
    tq = QUERY_TILE
    upper = lax.broadcasted_iota(jnp.int32, (tq, tq), 1) > lax.broadcasted_iota(
        jnp.int32, (tq, tq), 0
    )

    def scores(q, k_ref, low, high):
        return lax.dot_general(q, k_ref[low:high, :], dims, preferred_element_type=jnp.float32) * score_scale

    for tile in range(STRIDE // tq):
        low, high = tile * tq, (tile + 1) * tq
        q = q_ref[low:high, :]
        parts = []
        if with_prev:
            parts.append((jnp.where(upper, scores(q, kp_ref, low, high), -jnp.inf), vp_ref, low, high))
            if high < STRIDE:
                parts.append((scores(q, kp_ref, high, STRIDE), vp_ref, high, STRIDE))
        if low > 0:
            parts.append((scores(q, kc_ref, 0, low), vc_ref, 0, low))
        parts.append((jnp.where(upper, -jnp.inf, scores(q, kc_ref, low, high)), vc_ref, low, high))
        maxima = functools.reduce(
            jnp.maximum, [jnp.max(p[0], axis=1, keepdims=True) for p in parts]
        )
        expos = [jnp.exp(p[0] - maxima) for p in parts]
        total = functools.reduce(jnp.add, [jnp.sum(e, axis=1, keepdims=True) for e in expos])
        inverse = 1.0 / total
        out = None
        for e, (_, v_ref, a, b) in zip(expos, parts):
            term = jnp.dot((e * inverse).astype(jnp.bfloat16), v_ref[a:b, :], preferred_element_type=jnp.float32)
            out = term if out is None else out + term
        o_ref[low:high, :] = out.astype(o_ref.dtype)


def row_kernel(flag_ref, *refs):
    has_prev = flag_ref[0] > 0

    @pl.when(has_prev)
    def _():
        row_tiles(True, *refs)

    @pl.when(jnp.logical_not(has_prev))
    def _():
        row_tiles(False, *refs)


def attend_rows(has_prev, queries, prev_pair, keys, values):
    tokens, width = queries.shape
    heads = width // DH
    spec = pl.BlockSpec((STRIDE, DH), lambda h, flag: (0, h))
    prev_key_spec = pl.BlockSpec((None, STRIDE, DH), lambda h, flag: (0, 0, h))
    prev_value_spec = pl.BlockSpec((None, STRIDE, DH), lambda h, flag: (1, 0, h))
    scores = heads * tokens * (STRIDE + QUERY_TILE)
    return pl.pallas_call(
        row_kernel,
        out_shape=jax.ShapeDtypeStruct((2, tokens, width), jnp.bfloat16),
        grid_spec=pltpu.PrefetchScalarGridSpec(
            num_scalar_prefetch=1,
            grid=(heads,),
            in_specs=[spec, prev_key_spec, spec, prev_value_spec, spec],
            out_specs=prev_key_spec,
        ),
        cost_estimate=pl.CostEstimate(
            flops=4 * scores * DH, transcendentals=scores, bytes_accessed=6 * tokens * width * 2
        ),
    )(has_prev, queries, prev_pair, keys, prev_pair, values)


def local(query_vectors, key_vectors, value_vectors):
    local_tokens = query_vectors.shape[1]
    feature_width = query_vectors.shape[2]
    heads_here = feature_width // DH
    assert local_tokens == STRIDE
    blocks = lax.axis_size("seq")
    width = STRIDE // blocks
    seq_index = lax.axis_index("seq")
    prev_pair = shifted(jnp.stack([key_vectors[0], value_vectors[0]]), "seq", 1)
    stacked = jnp.stack(
        [
            query_vectors[1].reshape(blocks, width, feature_width),
            key_vectors[1].reshape(blocks, width, feature_width),
            value_vectors[1].reshape(blocks, width, feature_width),
        ],
        axis=1,
    )
    moved = lax.all_to_all(stacked, "seq", split_axis=0, concat_axis=0, tiled=True)
    _, prev_pair = lax.optimization_barrier((moved, prev_pair))
    grid = moved.reshape(blocks, 3, width, heads_here, DH)
    result = attend_columns(grid[:, 0], grid[:, 1], grid[:, 2])
    context = lax.all_to_all(
        result.reshape(blocks, width, feature_width), "seq", split_axis=0, concat_axis=0, tiled=True
    )
    column_out = context.reshape(local_tokens, feature_width)
    has_prev = (seq_index > 0).astype(jnp.int32).reshape(1)
    both = attend_rows(has_prev, query_vectors[0], prev_pair, key_vectors[0], value_vectors[0])
    return both.at[1].set(column_out)


def solution(mesh):
    return jax.shard_map(
        local,
        mesh=mesh,
        in_specs=(
            P(None, ("groups", "seq"), "head"),
            P(None, ("groups", "seq"), "head"),
            P(None, ("groups", "seq"), "head"),
        ),
        out_specs=P(None, ("groups", "seq"), "head"),
        check_vma=False,
    )
```

```python
import functools
import math

import jax
import jax.numpy as jnp
from jax import lax
from jax.experimental import pallas as pl
from jax.experimental.pallas import tpu as pltpu
from jax.sharding import PartitionSpec as P

DH = 128
STRIDE = 1024
QUERY_TILE = 256


def shifted(block, axis, distance):
    devices = range(lax.axis_size(axis))
    route = [(i - distance, i) for i in devices if i - distance in devices]
    return lax.ppermute(block, axis, route)


def attend_columns(query_cols, key_cols, value_cols):
    score_scale = 1.0 / math.sqrt(DH)
    scores = (
        jnp.einsum("rchd,schd->chrs", query_cols, key_cols, preferred_element_type=jnp.float32)
        * score_scale
    )
    count = query_cols.shape[0]
    row_pos = jnp.arange(count, dtype=jnp.int32)[:, None]
    other_pos = jnp.arange(count, dtype=jnp.int32)[None, :]
    allowed = other_pos <= row_pos
    scores = jnp.where(allowed[None, None], scores, -jnp.inf)
    maxima = jnp.max(scores, axis=-1, keepdims=True)
    expo = jnp.exp(scores - maxima)
    weights = (expo / jnp.sum(expo, axis=-1, keepdims=True)).astype(jnp.bfloat16)
    return jnp.einsum(
        "chrs,schd->rchd", weights, value_cols, preferred_element_type=jnp.float32
    ).astype(jnp.bfloat16)


def row_tiles(with_prev, q_ref, kp_ref, kc_ref, vp_ref, vc_ref, o_ref):
    score_scale = 1.0 / math.sqrt(DH)
    dims = (((1,), (1,)), ((), ()))
    tq = QUERY_TILE
    upper = lax.broadcasted_iota(jnp.int32, (tq, tq), 1) > lax.broadcasted_iota(
        jnp.int32, (tq, tq), 0
    )

    def scores(q, k_ref, low, high):
        return lax.dot_general(q, k_ref[low:high, :], dims, preferred_element_type=jnp.float32) * score_scale

    for tile in range(STRIDE // tq):
        low, high = tile * tq, (tile + 1) * tq
        q = q_ref[low:high, :]
        parts = []
        if with_prev:
            parts.append((jnp.where(upper, scores(q, kp_ref, low, high), -jnp.inf), vp_ref, low, high))
            if high < STRIDE:
                parts.append((scores(q, kp_ref, high, STRIDE), vp_ref, high, STRIDE))
        if low > 0:
            parts.append((scores(q, kc_ref, 0, low), vc_ref, 0, low))
        parts.append((jnp.where(upper, -jnp.inf, scores(q, kc_ref, low, high)), vc_ref, low, high))
        maxima = functools.reduce(
            jnp.maximum, [jnp.max(p[0], axis=1, keepdims=True) for p in parts]
        )
        expos = [jnp.exp(p[0] - maxima) for p in parts]
        total = functools.reduce(jnp.add, [jnp.sum(e, axis=1, keepdims=True) for e in expos])
        inverse = 1.0 / total
        out = None
        for e, (_, v_ref, a, b) in zip(expos, parts):
            term = jnp.dot((e * inverse).astype(jnp.bfloat16), v_ref[a:b, :], preferred_element_type=jnp.float32)
            out = term if out is None else out + term
        o_ref[low:high, :] = out.astype(o_ref.dtype)


def row_kernel(flag_ref, *refs):
    has_prev = flag_ref[0] > 0

    @pl.when(has_prev)
    def _():
        row_tiles(True, *refs)

    @pl.when(jnp.logical_not(has_prev))
    def _():
        row_tiles(False, *refs)


def attend_rows(has_prev, queries, prev_pair, keys, values):
    tokens, width = queries.shape
    heads = width // DH
    spec = pl.BlockSpec((STRIDE, DH), lambda h, flag: (0, h))
    prev_key_spec = pl.BlockSpec((None, STRIDE, DH), lambda h, flag: (0, 0, h))
    prev_value_spec = pl.BlockSpec((None, STRIDE, DH), lambda h, flag: (1, 0, h))
    scores = heads * tokens * (STRIDE + QUERY_TILE)
    return pl.pallas_call(
        row_kernel,
        out_shape=jax.ShapeDtypeStruct((2, tokens, width), jnp.bfloat16),
        grid_spec=pltpu.PrefetchScalarGridSpec(
            num_scalar_prefetch=1,
            grid=(heads,),
            in_specs=[spec, prev_key_spec, spec, prev_value_spec, spec],
            out_specs=prev_key_spec,
        ),
        cost_estimate=pl.CostEstimate(
            flops=4 * scores * DH, transcendentals=scores, bytes_accessed=6 * tokens * width * 2
        ),
    )(has_prev, queries, prev_pair, keys, prev_pair, values)


def pack_kernel(q_ref, k_ref, v_ref, kp_ref, vp_ref, o_ref, pair_ref):
    o_ref[0] = q_ref[...]
    o_ref[1] = k_ref[...]
    o_ref[2] = v_ref[...]
    pair_ref[0] = kp_ref[...]
    pair_ref[1] = vp_ref[...]


def pack(query_vectors, key_vectors, value_vectors, blocks):
    _, tokens, width = query_vectors.shape
    size = tokens // blocks
    column = pl.BlockSpec((None, size, width), lambda b: (1, b, 0))
    row = pl.BlockSpec((None, size, width), lambda b: (0, b, 0))
    return pl.pallas_call(
        pack_kernel,
        out_shape=(
            jax.ShapeDtypeStruct((blocks, 3, size, width), query_vectors.dtype),
            jax.ShapeDtypeStruct((2, tokens, width), query_vectors.dtype),
        ),
        grid=(blocks,),
        in_specs=[column, column, column, row, row],
        out_specs=(
            pl.BlockSpec((None, 3, size, width), lambda b: (b, 0, 0, 0)),
            pl.BlockSpec((2, size, width), lambda b: (0, b, 0)),
        ),
    )(query_vectors, key_vectors, value_vectors, key_vectors, value_vectors)


def local(query_vectors, key_vectors, value_vectors):
    local_tokens = query_vectors.shape[1]
    feature_width = query_vectors.shape[2]
    heads_here = feature_width // DH
    assert local_tokens == STRIDE
    blocks = lax.axis_size("seq")
    width = STRIDE // blocks
    seq_index = lax.axis_index("seq")
    if width % 16 == 0:
        stacked, pair = pack(query_vectors, key_vectors, value_vectors, blocks)
    else:
        pair = jnp.stack([key_vectors[0], value_vectors[0]])
        stacked = jnp.stack(
            [
                query_vectors[1].reshape(blocks, width, feature_width),
                key_vectors[1].reshape(blocks, width, feature_width),
                value_vectors[1].reshape(blocks, width, feature_width),
            ],
            axis=1,
        )
    prev_pair = shifted(pair, "seq", 1)
    moved = lax.all_to_all(stacked, "seq", split_axis=0, concat_axis=0, tiled=True)
    _, prev_pair = lax.optimization_barrier((moved, prev_pair))
    grid = moved.reshape(blocks, 3, width, heads_here, DH)
    result = attend_columns(grid[:, 0], grid[:, 1], grid[:, 2])
    context = lax.all_to_all(
        result.reshape(blocks, width, feature_width), "seq", split_axis=0, concat_axis=0, tiled=True
    )
    column_out = context.reshape(local_tokens, feature_width)
    has_prev = (seq_index > 0).astype(jnp.int32).reshape(1)
    both = attend_rows(has_prev, query_vectors[0], prev_pair, key_vectors[0], value_vectors[0])
    return both.at[1].set(column_out)


def solution(mesh):
    return jax.shard_map(
        local,
        mesh=mesh,
        in_specs=(
            P(None, ("groups", "seq"), "head"),
            P(None, ("groups", "seq"), "head"),
            P(None, ("groups", "seq"), "head"),
        ),
        out_specs=P(None, ("groups", "seq"), "head"),
        check_vma=False,
    )
```

```python
import functools
import math

import jax
import jax.numpy as jnp
from jax import lax
from jax.experimental import pallas as pl
from jax.experimental.pallas import tpu as pltpu
from jax.sharding import PartitionSpec as P

DH = 128
STRIDE = 1024
QUERY_TILE = 256


def shifted(block, axis, distance):
    devices = range(lax.axis_size(axis))
    route = [(i - distance, i) for i in devices if i - distance in devices]
    return lax.ppermute(block, axis, route)


def attend_columns(query_cols, key_cols, value_cols):
    score_scale = 1.0 / math.sqrt(DH)
    scores = (
        jnp.einsum("rchd,schd->chrs", query_cols, key_cols, preferred_element_type=jnp.float32)
        * score_scale
    )
    count = query_cols.shape[0]
    row_pos = jnp.arange(count, dtype=jnp.int32)[:, None]
    other_pos = jnp.arange(count, dtype=jnp.int32)[None, :]
    allowed = other_pos <= row_pos
    scores = jnp.where(allowed[None, None], scores, -jnp.inf)
    maxima = jnp.max(scores, axis=-1, keepdims=True)
    expo = jnp.exp(scores - maxima)
    weights = (expo / jnp.sum(expo, axis=-1, keepdims=True)).astype(jnp.bfloat16)
    return jnp.einsum(
        "chrs,schd->rchd", weights, value_cols, preferred_element_type=jnp.float32
    ).astype(jnp.bfloat16)


def row_tiles(with_prev, q_ref, kp_ref, kc_ref, vp_ref, vc_ref, o_ref):
    score_scale = 1.0 / math.sqrt(DH)
    dims = (((1,), (1,)), ((), ()))
    tq = QUERY_TILE
    upper = lax.broadcasted_iota(jnp.int32, (tq, tq), 1) > lax.broadcasted_iota(
        jnp.int32, (tq, tq), 0
    )

    def scores(q, k_ref, low, high):
        return lax.dot_general(q, k_ref[low:high, :], dims, preferred_element_type=jnp.float32) * score_scale

    for tile in range(STRIDE // tq):
        low, high = tile * tq, (tile + 1) * tq
        q = q_ref[low:high, :]
        parts = []
        if with_prev:
            parts.append((jnp.where(upper, scores(q, kp_ref, low, high), -jnp.inf), vp_ref, low, high))
            if high < STRIDE:
                parts.append((scores(q, kp_ref, high, STRIDE), vp_ref, high, STRIDE))
        if low > 0:
            parts.append((scores(q, kc_ref, 0, low), vc_ref, 0, low))
        parts.append((jnp.where(upper, -jnp.inf, scores(q, kc_ref, low, high)), vc_ref, low, high))
        maxima = functools.reduce(
            jnp.maximum, [jnp.max(p[0], axis=1, keepdims=True) for p in parts]
        )
        expos = [jnp.exp(p[0] - maxima) for p in parts]
        total = functools.reduce(jnp.add, [jnp.sum(e, axis=1, keepdims=True) for e in expos])
        inverse = 1.0 / total
        out = None
        for e, (_, v_ref, a, b) in zip(expos, parts):
            term = jnp.dot((e * inverse).astype(jnp.bfloat16), v_ref[a:b, :], preferred_element_type=jnp.float32)
            out = term if out is None else out + term
        o_ref[low:high, :] = out.astype(o_ref.dtype)


def row_kernel(flag_ref, *refs):
    has_prev = flag_ref[0] > 0

    @pl.when(has_prev)
    def _():
        row_tiles(True, *refs)

    @pl.when(jnp.logical_not(has_prev))
    def _():
        row_tiles(False, *refs)


def attend_rows(has_prev, queries, prev_pair, keys, values):
    tokens, width = queries.shape
    heads = width // DH
    spec = pl.BlockSpec((STRIDE, DH), lambda h, flag: (0, h))
    prev_key_spec = pl.BlockSpec((None, STRIDE, DH), lambda h, flag: (0, 0, h))
    prev_value_spec = pl.BlockSpec((None, STRIDE, DH), lambda h, flag: (1, 0, h))
    scores = heads * tokens * (STRIDE + QUERY_TILE)
    return pl.pallas_call(
        row_kernel,
        out_shape=jax.ShapeDtypeStruct((2, tokens, width), jnp.bfloat16),
        grid_spec=pltpu.PrefetchScalarGridSpec(
            num_scalar_prefetch=1,
            grid=(heads,),
            in_specs=[spec, prev_key_spec, spec, prev_value_spec, spec],
            out_specs=prev_key_spec,
        ),
        cost_estimate=pl.CostEstimate(
            flops=4 * scores * DH, transcendentals=scores, bytes_accessed=6 * tokens * width * 2
        ),
    )(has_prev, queries, prev_pair, keys, prev_pair, values)


def pack_kernel(q_ref, k_ref, v_ref, kp_ref, vp_ref, o_ref, pair_ref):
    shape = (o_ref.shape[0], o_ref.shape[2], o_ref.shape[3])
    o_ref[:, 0] = q_ref[...].reshape(shape)
    o_ref[:, 1] = k_ref[...].reshape(shape)
    o_ref[:, 2] = v_ref[...].reshape(shape)
    pair_ref[0] = kp_ref[...]
    pair_ref[1] = vp_ref[...]


def pack(query_vectors, key_vectors, value_vectors, blocks, steps=2):
    _, tokens, width = query_vectors.shape
    size = tokens // blocks
    rows = tokens // steps
    column = pl.BlockSpec((None, rows, width), lambda b: (1, b, 0))
    row = pl.BlockSpec((None, rows, width), lambda b: (0, b, 0))
    return pl.pallas_call(
        pack_kernel,
        out_shape=(
            jax.ShapeDtypeStruct((blocks, 3, size, width), query_vectors.dtype),
            jax.ShapeDtypeStruct((2, tokens, width), query_vectors.dtype),
        ),
        grid=(steps,),
        in_specs=[column, column, column, row, row],
        out_specs=(
            pl.BlockSpec((blocks // steps, 3, size, width), lambda b: (b, 0, 0, 0)),
            pl.BlockSpec((2, rows, width), lambda b: (0, b, 0)),
        ),
    )(query_vectors, key_vectors, value_vectors, key_vectors, value_vectors)


def local(query_vectors, key_vectors, value_vectors):
    local_tokens = query_vectors.shape[1]
    feature_width = query_vectors.shape[2]
    heads_here = feature_width // DH
    assert local_tokens == STRIDE
    blocks = lax.axis_size("seq")
    width = STRIDE // blocks
    seq_index = lax.axis_index("seq")
    if width % 16 == 0:
        stacked, pair = pack(query_vectors, key_vectors, value_vectors, blocks)
    else:
        pair = jnp.stack([key_vectors[0], value_vectors[0]])
        stacked = jnp.stack(
            [
                query_vectors[1].reshape(blocks, width, feature_width),
                key_vectors[1].reshape(blocks, width, feature_width),
                value_vectors[1].reshape(blocks, width, feature_width),
            ],
            axis=1,
        )
    prev_pair = shifted(pair, "seq", 1)
    moved = lax.all_to_all(stacked, "seq", split_axis=0, concat_axis=0, tiled=True)
    _, prev_pair = lax.optimization_barrier((moved, prev_pair))
    grid = moved.reshape(blocks, 3, width, heads_here, DH)
    result = attend_columns(grid[:, 0], grid[:, 1], grid[:, 2])
    context = lax.all_to_all(
        result.reshape(blocks, width, feature_width), "seq", split_axis=0, concat_axis=0, tiled=True
    )
    column_out = context.reshape(local_tokens, feature_width)
    has_prev = (seq_index > 0).astype(jnp.int32).reshape(1)
    both = attend_rows(has_prev, query_vectors[0], prev_pair, key_vectors[0], value_vectors[0])
    return both.at[1].set(column_out)


def solution(mesh):
    return jax.shard_map(
        local,
        mesh=mesh,
        in_specs=(
            P(None, ("groups", "seq"), "head"),
            P(None, ("groups", "seq"), "head"),
            P(None, ("groups", "seq"), "head"),
        ),
        out_specs=P(None, ("groups", "seq"), "head"),
        check_vma=False,
    )
```

```python
import functools
import math

import jax
import jax.numpy as jnp
from jax import lax
from jax.experimental import pallas as pl
from jax.experimental.pallas import tpu as pltpu
from jax.sharding import PartitionSpec as P

DH = 128
STRIDE = 1024
QUERY_TILE = 256


def shifted(block, axis, distance):
    devices = range(lax.axis_size(axis))
    route = [(i - distance, i) for i in devices if i - distance in devices]
    return lax.ppermute(block, axis, route)


def attend_columns(query_cols, key_cols, value_cols):
    score_scale = 1.0 / math.sqrt(DH)
    scores = (
        jnp.einsum("rchd,schd->chrs", query_cols, key_cols, preferred_element_type=jnp.float32)
        * score_scale
    )
    count = query_cols.shape[0]
    row_pos = jnp.arange(count, dtype=jnp.int32)[:, None]
    other_pos = jnp.arange(count, dtype=jnp.int32)[None, :]
    allowed = other_pos <= row_pos
    scores = jnp.where(allowed[None, None], scores, -jnp.inf)
    maxima = jnp.max(scores, axis=-1, keepdims=True)
    expo = jnp.exp(scores - maxima)
    weights = (expo / jnp.sum(expo, axis=-1, keepdims=True)).astype(jnp.bfloat16)
    return jnp.einsum(
        "chrs,schd->rchd", weights, value_cols, preferred_element_type=jnp.float32
    ).astype(jnp.bfloat16)


def row_tiles(with_prev, q_ref, kp_ref, kc_ref, vp_ref, vc_ref, o_ref):
    score_scale = 1.0 / math.sqrt(DH)
    dims = (((1,), (1,)), ((), ()))
    tq = QUERY_TILE
    upper = lax.broadcasted_iota(jnp.int32, (tq, tq), 1) > lax.broadcasted_iota(
        jnp.int32, (tq, tq), 0
    )

    def scores(q, k_ref, low, high):
        return lax.dot_general(q, k_ref[low:high, :], dims, preferred_element_type=jnp.float32)

    for tile in range(STRIDE // tq):
        low, high = tile * tq, (tile + 1) * tq
        q = q_ref[low:high, :]
        parts = []
        if with_prev:
            parts.append((jnp.where(upper, scores(q, kp_ref, low, high), -jnp.inf), vp_ref, low, high))
            if high < STRIDE:
                parts.append((scores(q, kp_ref, high, STRIDE), vp_ref, high, STRIDE))
        if low > 0:
            parts.append((scores(q, kc_ref, 0, low), vc_ref, 0, low))
        parts.append((jnp.where(upper, -jnp.inf, scores(q, kc_ref, low, high)), vc_ref, low, high))
        maxima = functools.reduce(
            jnp.maximum, [jnp.max(p[0], axis=1, keepdims=True) for p in parts]
        )
        expos = [jnp.exp2((p[0] - maxima) * (score_scale * math.log2(math.e))) for p in parts]
        total = functools.reduce(jnp.add, [jnp.sum(e, axis=1, keepdims=True) for e in expos])
        inverse = 1.0 / total
        out = None
        for e, (_, v_ref, a, b) in zip(expos, parts):
            term = jnp.dot((e * inverse).astype(jnp.bfloat16), v_ref[a:b, :], preferred_element_type=jnp.float32)
            out = term if out is None else out + term
        o_ref[low:high, :] = out.astype(o_ref.dtype)


def row_kernel(flag_ref, *refs):
    has_prev = flag_ref[0] > 0

    @pl.when(has_prev)
    def _():
        row_tiles(True, *refs)

    @pl.when(jnp.logical_not(has_prev))
    def _():
        row_tiles(False, *refs)


def attend_rows(has_prev, queries, prev_pair, keys, values):
    tokens, width = queries.shape
    heads = width // DH
    spec = pl.BlockSpec((STRIDE, DH), lambda h, flag: (0, h))
    prev_key_spec = pl.BlockSpec((None, STRIDE, DH), lambda h, flag: (0, 0, h))
    prev_value_spec = pl.BlockSpec((None, STRIDE, DH), lambda h, flag: (1, 0, h))
    scores = heads * tokens * (STRIDE + QUERY_TILE)
    return pl.pallas_call(
        row_kernel,
        out_shape=jax.ShapeDtypeStruct((2, tokens, width), jnp.bfloat16),
        grid_spec=pltpu.PrefetchScalarGridSpec(
            num_scalar_prefetch=1,
            grid=(heads,),
            in_specs=[spec, prev_key_spec, spec, prev_value_spec, spec],
            out_specs=prev_key_spec,
        ),
        cost_estimate=pl.CostEstimate(
            flops=4 * scores * DH, transcendentals=scores, bytes_accessed=6 * tokens * width * 2
        ),
    )(has_prev, queries, prev_pair, keys, prev_pair, values)


def pack_kernel(q_ref, k_ref, v_ref, kp_ref, vp_ref, o_ref, pair_ref):
    shape = (o_ref.shape[0], o_ref.shape[2], o_ref.shape[3])
    o_ref[:, 0] = q_ref[...].reshape(shape)
    o_ref[:, 1] = k_ref[...].reshape(shape)
    o_ref[:, 2] = v_ref[...].reshape(shape)
    pair_ref[0] = kp_ref[...]
    pair_ref[1] = vp_ref[...]


def pack(query_vectors, key_vectors, value_vectors, blocks, steps=2):
    _, tokens, width = query_vectors.shape
    size = tokens // blocks
    rows = tokens // steps
    column = pl.BlockSpec((None, rows, width), lambda b: (1, b, 0))
    row = pl.BlockSpec((None, rows, width), lambda b: (0, b, 0))
    return pl.pallas_call(
        pack_kernel,
        out_shape=(
            jax.ShapeDtypeStruct((blocks, 3, size, width), query_vectors.dtype),
            jax.ShapeDtypeStruct((2, tokens, width), query_vectors.dtype),
        ),
        grid=(steps,),
        in_specs=[column, column, column, row, row],
        out_specs=(
            pl.BlockSpec((blocks // steps, 3, size, width), lambda b: (b, 0, 0, 0)),
            pl.BlockSpec((2, rows, width), lambda b: (0, b, 0)),
        ),
    )(query_vectors, key_vectors, value_vectors, key_vectors, value_vectors)


def local(query_vectors, key_vectors, value_vectors):
    local_tokens = query_vectors.shape[1]
    feature_width = query_vectors.shape[2]
    heads_here = feature_width // DH
    assert local_tokens == STRIDE
    blocks = lax.axis_size("seq")
    width = STRIDE // blocks
    seq_index = lax.axis_index("seq")
    if width % 16 == 0:
        stacked, pair = pack(query_vectors, key_vectors, value_vectors, blocks)
    else:
        pair = jnp.stack([key_vectors[0], value_vectors[0]])
        stacked = jnp.stack(
            [
                query_vectors[1].reshape(blocks, width, feature_width),
                key_vectors[1].reshape(blocks, width, feature_width),
                value_vectors[1].reshape(blocks, width, feature_width),
            ],
            axis=1,
        )
    prev_pair = shifted(pair, "seq", 1)
    moved = lax.all_to_all(stacked, "seq", split_axis=0, concat_axis=0, tiled=True)
    _, prev_pair = lax.optimization_barrier((moved, prev_pair))
    grid = moved.reshape(blocks, 3, width, heads_here, DH)
    result = attend_columns(grid[:, 0], grid[:, 1], grid[:, 2])
    context = lax.all_to_all(
        result.reshape(blocks, width, feature_width), "seq", split_axis=0, concat_axis=0, tiled=True
    )
    column_out = context.reshape(local_tokens, feature_width)
    has_prev = (seq_index > 0).astype(jnp.int32).reshape(1)
    both = attend_rows(has_prev, query_vectors[0], prev_pair, key_vectors[0], value_vectors[0])
    return both.at[1].set(column_out)


def solution(mesh):
    return jax.shard_map(
        local,
        mesh=mesh,
        in_specs=(
            P(None, ("groups", "seq"), "head"),
            P(None, ("groups", "seq"), "head"),
            P(None, ("groups", "seq"), "head"),
        ),
        out_specs=P(None, ("groups", "seq"), "head"),
        check_vma=False,
    )
```

```python
import functools
import math

import jax
import jax.numpy as jnp
from jax import lax
from jax.experimental import pallas as pl
from jax.experimental.pallas import tpu as pltpu
from jax.sharding import PartitionSpec as P

DH = 128
STRIDE = 1024
QUERY_TILE = 256


def shifted(block, axis, distance):
    devices = range(lax.axis_size(axis))
    route = [(i - distance, i) for i in devices if i - distance in devices]
    return lax.ppermute(block, axis, route)


def attend_columns(query_cols, key_cols, value_cols):
    score_scale = 1.0 / math.sqrt(DH)
    scores = (
        jnp.einsum("rchd,schd->chrs", query_cols, key_cols, preferred_element_type=jnp.float32)
        * score_scale
    )
    count = query_cols.shape[0]
    row_pos = jnp.arange(count, dtype=jnp.int32)[:, None]
    other_pos = jnp.arange(count, dtype=jnp.int32)[None, :]
    allowed = other_pos <= row_pos
    scores = jnp.where(allowed[None, None], scores, -jnp.inf)
    maxima = jnp.max(scores, axis=-1, keepdims=True)
    expo = jnp.exp(scores - maxima)
    weights = (expo / jnp.sum(expo, axis=-1, keepdims=True)).astype(jnp.bfloat16)
    return jnp.einsum(
        "chrs,schd->rchd", weights, value_cols, preferred_element_type=jnp.float32
    ).astype(jnp.bfloat16)


def row_tiles(with_prev, q_ref, kp_ref, kc_ref, vp_ref, vc_ref, o_ref):
    score_scale = 1.0 / math.sqrt(DH)
    dims = (((1,), (1,)), ((), ()))
    tq = QUERY_TILE
    upper = lax.broadcasted_iota(jnp.int32, (tq, tq), 1) > lax.broadcasted_iota(
        jnp.int32, (tq, tq), 0
    )

    def scores(q, k_ref, low, high):
        return lax.dot_general(q, k_ref[low:high, :], dims, preferred_element_type=jnp.float32)

    for tile in range(STRIDE // tq):
        low, high = tile * tq, (tile + 1) * tq
        q = q_ref[low:high, :]
        parts = []
        if with_prev:
            parts.append((jnp.where(upper, scores(q, kp_ref, low, high), -jnp.inf), vp_ref, low, high))
            if high < STRIDE:
                parts.append((scores(q, kp_ref, high, STRIDE), vp_ref, high, STRIDE))
        if low > 0:
            parts.append((scores(q, kc_ref, 0, low), vc_ref, 0, low))
        parts.append((jnp.where(upper, -jnp.inf, scores(q, kc_ref, low, high)), vc_ref, low, high))
        maxima = functools.reduce(
            jnp.maximum, [jnp.max(p[0], axis=1, keepdims=True) for p in parts]
        )
        expos = [jnp.exp2((p[0] - maxima) * (score_scale * math.log2(math.e))) for p in parts]
        total = functools.reduce(jnp.add, [jnp.sum(e, axis=1, keepdims=True) for e in expos])
        inverse = 1.0 / total
        out = None
        for e, (_, v_ref, a, b) in zip(expos, parts):
            term = jnp.dot((e * inverse).astype(jnp.bfloat16), v_ref[a:b, :], preferred_element_type=jnp.float32)
            out = term if out is None else out + term
        o_ref[low:high, :] = out.astype(o_ref.dtype)


def row_kernel(flag_ref, *refs):
    has_prev = flag_ref[0] > 0

    @pl.when(has_prev)
    def _():
        row_tiles(True, *refs)

    @pl.when(jnp.logical_not(has_prev))
    def _():
        row_tiles(False, *refs)


def attend_rows(has_prev, queries, prev_pair, keys, values):
    tokens, width = queries.shape
    heads = width // DH
    spec = pl.BlockSpec((STRIDE, DH), lambda h, flag: (0, h))
    prev_key_spec = pl.BlockSpec((None, STRIDE, DH), lambda h, flag: (0, 0, h))
    prev_value_spec = pl.BlockSpec((None, STRIDE, DH), lambda h, flag: (1, 0, h))
    scores = heads * tokens * (STRIDE + QUERY_TILE)
    return pl.pallas_call(
        row_kernel,
        out_shape=jax.ShapeDtypeStruct((2, tokens, width), jnp.bfloat16),
        grid_spec=pltpu.PrefetchScalarGridSpec(
            num_scalar_prefetch=1,
            grid=(heads,),
            in_specs=[spec, prev_key_spec, spec, prev_value_spec, spec],
            out_specs=prev_key_spec,
        ),
        cost_estimate=pl.CostEstimate(
            flops=4 * scores * DH, transcendentals=scores, bytes_accessed=6 * tokens * width * 2
        ),
    )(has_prev, queries, prev_pair, keys, prev_pair, values)


def pack_kernel(q_ref, k_ref, v_ref, kp_ref, vp_ref, o_ref, pair_ref):
    shape = (o_ref.shape[0], o_ref.shape[2], o_ref.shape[3])
    o_ref[:, 0] = q_ref[...].reshape(shape)
    o_ref[:, 1] = k_ref[...].reshape(shape)
    o_ref[:, 2] = v_ref[...].reshape(shape)
    pair_ref[0] = kp_ref[...]
    pair_ref[1] = vp_ref[...]


def pack(query_vectors, key_vectors, value_vectors, blocks, steps=2):
    _, tokens, width = query_vectors.shape
    size = tokens // blocks
    rows = tokens // steps
    column = pl.BlockSpec((None, rows, width), lambda b: (1, b, 0))
    row = pl.BlockSpec((None, rows, width), lambda b: (0, b, 0))
    return pl.pallas_call(
        pack_kernel,
        out_shape=(
            jax.ShapeDtypeStruct((blocks, 3, size, width), query_vectors.dtype),
            jax.ShapeDtypeStruct((steps, 2, rows, width), query_vectors.dtype),
        ),
        grid=(steps,),
        in_specs=[column, column, column, row, row],
        out_specs=(
            pl.BlockSpec((blocks // steps, 3, size, width), lambda b: (b, 0, 0, 0)),
            pl.BlockSpec((None, 2, rows, width), lambda b: (b, 0, 0, 0)),
        ),
    )(query_vectors, key_vectors, value_vectors, key_vectors, value_vectors)


def local(query_vectors, key_vectors, value_vectors):
    local_tokens = query_vectors.shape[1]
    feature_width = query_vectors.shape[2]
    heads_here = feature_width // DH
    assert local_tokens == STRIDE
    blocks = lax.axis_size("seq")
    width = STRIDE // blocks
    seq_index = lax.axis_index("seq")
    half_rows = STRIDE // 2
    if width % 16 == 0:
        stacked, pair = pack(query_vectors, key_vectors, value_vectors, blocks)
    else:
        pair = jnp.stack([key_vectors[0], value_vectors[0]]).reshape(2, 2, half_rows, feature_width)
        pair = jnp.moveaxis(pair, 1, 0)
        stacked = jnp.stack(
            [
                query_vectors[1].reshape(blocks, width, feature_width),
                key_vectors[1].reshape(blocks, width, feature_width),
                value_vectors[1].reshape(blocks, width, feature_width),
            ],
            axis=1,
        )
    first_half = shifted(pair[0], "seq", 1)
    second_direct = lax.ppermute(pair[1], "seq", [(i, i + 1) for i in range(0, blocks - 1, 2)])
    second_out = lax.ppermute(pair[1], "seq", [(i, i + 2) for i in range(1, blocks - 2, 2)])
    second_relay = lax.ppermute(second_out, "seq", [(i, i - 1) for i in range(3, blocks, 2)])
    moved = lax.all_to_all(stacked, "seq", split_axis=0, concat_axis=0, tiled=True)
    _, first_half, second_direct, second_relay = lax.optimization_barrier(
        (moved, first_half, second_direct, second_relay)
    )
    second_half = jnp.where(seq_index % 2 == 1, second_direct, second_relay)
    prev_pair = jnp.concatenate([first_half, second_half], axis=1)
    grid = moved.reshape(blocks, 3, width, heads_here, DH)
    result = attend_columns(grid[:, 0], grid[:, 1], grid[:, 2])
    context = lax.all_to_all(
        result.reshape(blocks, width, feature_width), "seq", split_axis=0, concat_axis=0, tiled=True
    )
    column_out = context.reshape(local_tokens, feature_width)
    has_prev = (seq_index > 0).astype(jnp.int32).reshape(1)
    both = attend_rows(has_prev, query_vectors[0], prev_pair, key_vectors[0], value_vectors[0])
    return both.at[1].set(column_out)


def solution(mesh):
    return jax.shard_map(
        local,
        mesh=mesh,
        in_specs=(
            P(None, ("groups", "seq"), "head"),
            P(None, ("groups", "seq"), "head"),
            P(None, ("groups", "seq"), "head"),
        ),
        out_specs=P(None, ("groups", "seq"), "head"),
        check_vma=False,
    )
```

```python
import functools
import math

import jax
import jax.numpy as jnp
from jax import lax
from jax.experimental import pallas as pl
from jax.experimental.pallas import tpu as pltpu
from jax.sharding import PartitionSpec as P

DH = 128
STRIDE = 1024
QUERY_TILE = 128


def shifted(block, axis, distance):
    devices = range(lax.axis_size(axis))
    route = [(i - distance, i) for i in devices if i - distance in devices]
    return lax.ppermute(block, axis, route)


def attend_columns(query_cols, key_cols, value_cols):
    score_scale = 1.0 / math.sqrt(DH)
    scores = (
        jnp.einsum("rchd,schd->chrs", query_cols, key_cols, preferred_element_type=jnp.float32)
        * score_scale
    )
    count = query_cols.shape[0]
    row_pos = jnp.arange(count, dtype=jnp.int32)[:, None]
    other_pos = jnp.arange(count, dtype=jnp.int32)[None, :]
    allowed = other_pos <= row_pos
    scores = jnp.where(allowed[None, None], scores, -jnp.inf)
    maxima = jnp.max(scores, axis=-1, keepdims=True)
    expo = jnp.exp(scores - maxima)
    weights = (expo / jnp.sum(expo, axis=-1, keepdims=True)).astype(jnp.bfloat16)
    return jnp.einsum(
        "chrs,schd->rchd", weights, value_cols, preferred_element_type=jnp.float32
    ).astype(jnp.bfloat16)


def row_tiles(with_prev, q_ref, kp_ref, kc_ref, vp_ref, vc_ref, o_ref):
    score_scale = 1.0 / math.sqrt(DH)
    dims = (((1,), (1,)), ((), ()))
    tq = QUERY_TILE
    upper = lax.broadcasted_iota(jnp.int32, (tq, tq), 1) > lax.broadcasted_iota(
        jnp.int32, (tq, tq), 0
    )

    def scores(q, k_ref, low, high):
        return lax.dot_general(q, k_ref[low:high, :], dims, preferred_element_type=jnp.float32)

    for tile in range(STRIDE // tq):
        low, high = tile * tq, (tile + 1) * tq
        q = q_ref[low:high, :]
        parts = []
        if with_prev:
            parts.append((jnp.where(upper, scores(q, kp_ref, low, high), -jnp.inf), vp_ref, low, high))
            if high < STRIDE:
                parts.append((scores(q, kp_ref, high, STRIDE), vp_ref, high, STRIDE))
        if low > 0:
            parts.append((scores(q, kc_ref, 0, low), vc_ref, 0, low))
        parts.append((jnp.where(upper, -jnp.inf, scores(q, kc_ref, low, high)), vc_ref, low, high))
        maxima = functools.reduce(
            jnp.maximum, [jnp.max(p[0], axis=1, keepdims=True) for p in parts]
        )
        expos = [jnp.exp2((p[0] - maxima) * (score_scale * math.log2(math.e))) for p in parts]
        total = functools.reduce(jnp.add, [jnp.sum(e, axis=1, keepdims=True) for e in expos])
        inverse = 1.0 / total
        out = None
        for e, (_, v_ref, a, b) in zip(expos, parts):
            term = jnp.dot((e * inverse).astype(jnp.bfloat16), v_ref[a:b, :], preferred_element_type=jnp.float32)
            out = term if out is None else out + term
        o_ref[low:high, :] = out.astype(o_ref.dtype)


def row_kernel(flag_ref, *refs):
    has_prev = flag_ref[0] > 0

    @pl.when(has_prev)
    def _():
        row_tiles(True, *refs)

    @pl.when(jnp.logical_not(has_prev))
    def _():
        row_tiles(False, *refs)


def attend_rows(has_prev, queries, prev_pair, keys, values):
    tokens, width = queries.shape
    heads = width // DH
    spec = pl.BlockSpec((STRIDE, DH), lambda h, flag: (0, h))
    prev_key_spec = pl.BlockSpec((None, STRIDE, DH), lambda h, flag: (0, 0, h))
    prev_value_spec = pl.BlockSpec((None, STRIDE, DH), lambda h, flag: (1, 0, h))
    scores = heads * tokens * (STRIDE + QUERY_TILE)
    return pl.pallas_call(
        row_kernel,
        out_shape=jax.ShapeDtypeStruct((2, tokens, width), jnp.bfloat16),
        grid_spec=pltpu.PrefetchScalarGridSpec(
            num_scalar_prefetch=1,
            grid=(heads,),
            in_specs=[spec, prev_key_spec, spec, prev_value_spec, spec],
            out_specs=prev_key_spec,
        ),
        cost_estimate=pl.CostEstimate(
            flops=4 * scores * DH, transcendentals=scores, bytes_accessed=6 * tokens * width * 2
        ),
    )(has_prev, queries, prev_pair, keys, prev_pair, values)


def pack_kernel(q_ref, k_ref, v_ref, kp_ref, vp_ref, o_ref, pair_ref):
    shape = (o_ref.shape[0], o_ref.shape[2], o_ref.shape[3])
    o_ref[:, 0] = q_ref[...].reshape(shape)
    o_ref[:, 1] = k_ref[...].reshape(shape)
    o_ref[:, 2] = v_ref[...].reshape(shape)
    pair_ref[0] = kp_ref[...]
    pair_ref[1] = vp_ref[...]


def pack(query_vectors, key_vectors, value_vectors, blocks, steps=2):
    _, tokens, width = query_vectors.shape
    size = tokens // blocks
    rows = tokens // steps
    column = pl.BlockSpec((None, rows, width), lambda b: (1, b, 0))
    row = pl.BlockSpec((None, rows, width), lambda b: (0, b, 0))
    return pl.pallas_call(
        pack_kernel,
        out_shape=(
            jax.ShapeDtypeStruct((blocks, 3, size, width), query_vectors.dtype),
            jax.ShapeDtypeStruct((2, tokens, width), query_vectors.dtype),
        ),
        grid=(steps,),
        in_specs=[column, column, column, row, row],
        out_specs=(
            pl.BlockSpec((blocks // steps, 3, size, width), lambda b: (b, 0, 0, 0)),
            pl.BlockSpec((2, rows, width), lambda b: (0, b, 0)),
        ),
    )(query_vectors, key_vectors, value_vectors, key_vectors, value_vectors)


def local(query_vectors, key_vectors, value_vectors):
    local_tokens = query_vectors.shape[1]
    feature_width = query_vectors.shape[2]
    heads_here = feature_width // DH
    assert local_tokens == STRIDE
    blocks = lax.axis_size("seq")
    width = STRIDE // blocks
    seq_index = lax.axis_index("seq")
    if width % 16 == 0:
        stacked, pair = pack(query_vectors, key_vectors, value_vectors, blocks)
    else:
        pair = jnp.stack([key_vectors[0], value_vectors[0]])
        stacked = jnp.stack(
            [
                query_vectors[1].reshape(blocks, width, feature_width),
                key_vectors[1].reshape(blocks, width, feature_width),
                value_vectors[1].reshape(blocks, width, feature_width),
            ],
            axis=1,
        )
    prev_pair = shifted(pair, "seq", 1)
    moved = lax.all_to_all(stacked, "seq", split_axis=0, concat_axis=0, tiled=True)
    _, prev_pair = lax.optimization_barrier((moved, prev_pair))
    grid = moved.reshape(blocks, 3, width, heads_here, DH)
    result = attend_columns(grid[:, 0], grid[:, 1], grid[:, 2])
    context = lax.all_to_all(
        result.reshape(blocks, width, feature_width), "seq", split_axis=0, concat_axis=0, tiled=True
    )
    column_out = context.reshape(local_tokens, feature_width)
    has_prev = (seq_index > 0).astype(jnp.int32).reshape(1)
    both = attend_rows(has_prev, query_vectors[0], prev_pair, key_vectors[0], value_vectors[0])
    return both.at[1].set(column_out)


def solution(mesh):
    return jax.shard_map(
        local,
        mesh=mesh,
        in_specs=(
            P(None, ("groups", "seq"), "head"),
            P(None, ("groups", "seq"), "head"),
            P(None, ("groups", "seq"), "head"),
        ),
        out_specs=P(None, ("groups", "seq"), "head"),
        check_vma=False,
    )
```

```python
import functools
import math

import jax
import jax.numpy as jnp
from jax import lax
from jax.experimental import pallas as pl
from jax.experimental.pallas import tpu as pltpu
from jax.sharding import PartitionSpec as P

DH = 128
STRIDE = 1024
QUERY_TILE = 512


def shifted(block, axis, distance):
    devices = range(lax.axis_size(axis))
    route = [(i - distance, i) for i in devices if i - distance in devices]
    return lax.ppermute(block, axis, route)


def attend_columns(query_cols, key_cols, value_cols):
    score_scale = 1.0 / math.sqrt(DH)
    scores = (
        jnp.einsum("rchd,schd->chrs", query_cols, key_cols, preferred_element_type=jnp.float32)
        * score_scale
    )
    count = query_cols.shape[0]
    row_pos = jnp.arange(count, dtype=jnp.int32)[:, None]
    other_pos = jnp.arange(count, dtype=jnp.int32)[None, :]
    allowed = other_pos <= row_pos
    scores = jnp.where(allowed[None, None], scores, -jnp.inf)
    maxima = jnp.max(scores, axis=-1, keepdims=True)
    expo = jnp.exp(scores - maxima)
    weights = (expo / jnp.sum(expo, axis=-1, keepdims=True)).astype(jnp.bfloat16)
    return jnp.einsum(
        "chrs,schd->rchd", weights, value_cols, preferred_element_type=jnp.float32
    ).astype(jnp.bfloat16)


def row_tiles(with_prev, q_ref, kp_ref, kc_ref, vp_ref, vc_ref, o_ref):
    score_scale = 1.0 / math.sqrt(DH)
    dims = (((1,), (1,)), ((), ()))
    tq = QUERY_TILE
    upper = lax.broadcasted_iota(jnp.int32, (tq, tq), 1) > lax.broadcasted_iota(
        jnp.int32, (tq, tq), 0
    )

    def scores(q, k_ref, low, high):
        return lax.dot_general(q, k_ref[low:high, :], dims, preferred_element_type=jnp.float32)

    for tile in range(STRIDE // tq):
        low, high = tile * tq, (tile + 1) * tq
        q = q_ref[low:high, :]
        parts = []
        if with_prev:
            parts.append((jnp.where(upper, scores(q, kp_ref, low, high), -jnp.inf), vp_ref, low, high))
            if high < STRIDE:
                parts.append((scores(q, kp_ref, high, STRIDE), vp_ref, high, STRIDE))
        if low > 0:
            parts.append((scores(q, kc_ref, 0, low), vc_ref, 0, low))
        parts.append((jnp.where(upper, -jnp.inf, scores(q, kc_ref, low, high)), vc_ref, low, high))
        maxima = functools.reduce(
            jnp.maximum, [jnp.max(p[0], axis=1, keepdims=True) for p in parts]
        )
        expos = [jnp.exp2((p[0] - maxima) * (score_scale * math.log2(math.e))) for p in parts]
        total = functools.reduce(jnp.add, [jnp.sum(e, axis=1, keepdims=True) for e in expos])
        inverse = 1.0 / total
        out = None
        for e, (_, v_ref, a, b) in zip(expos, parts):
            term = jnp.dot((e * inverse).astype(jnp.bfloat16), v_ref[a:b, :], preferred_element_type=jnp.float32)
            out = term if out is None else out + term
        o_ref[low:high, :] = out.astype(o_ref.dtype)


def row_kernel(flag_ref, *refs):
    has_prev = flag_ref[0] > 0

    @pl.when(has_prev)
    def _():
        row_tiles(True, *refs)

    @pl.when(jnp.logical_not(has_prev))
    def _():
        row_tiles(False, *refs)


def attend_rows(has_prev, queries, prev_pair, keys, values):
    tokens, width = queries.shape
    heads = width // DH
    spec = pl.BlockSpec((STRIDE, DH), lambda h, flag: (0, h))
    prev_key_spec = pl.BlockSpec((None, STRIDE, DH), lambda h, flag: (0, 0, h))
    prev_value_spec = pl.BlockSpec((None, STRIDE, DH), lambda h, flag: (1, 0, h))
    scores = heads * tokens * (STRIDE + QUERY_TILE)
    return pl.pallas_call(
        row_kernel,
        out_shape=jax.ShapeDtypeStruct((2, tokens, width), jnp.bfloat16),
        grid_spec=pltpu.PrefetchScalarGridSpec(
            num_scalar_prefetch=1,
            grid=(heads,),
            in_specs=[spec, prev_key_spec, spec, prev_value_spec, spec],
            out_specs=prev_key_spec,
        ),
        cost_estimate=pl.CostEstimate(
            flops=4 * scores * DH, transcendentals=scores, bytes_accessed=6 * tokens * width * 2
        ),
    )(has_prev, queries, prev_pair, keys, prev_pair, values)


def pack_kernel(q_ref, k_ref, v_ref, kp_ref, vp_ref, o_ref, pair_ref):
    shape = (o_ref.shape[0], o_ref.shape[2], o_ref.shape[3])
    o_ref[:, 0] = q_ref[...].reshape(shape)
    o_ref[:, 1] = k_ref[...].reshape(shape)
    o_ref[:, 2] = v_ref[...].reshape(shape)
    pair_ref[0] = kp_ref[...]
    pair_ref[1] = vp_ref[...]


def pack(query_vectors, key_vectors, value_vectors, blocks, steps=2):
    _, tokens, width = query_vectors.shape
    size = tokens // blocks
    rows = tokens // steps
    column = pl.BlockSpec((None, rows, width), lambda b: (1, b, 0))
    row = pl.BlockSpec((None, rows, width), lambda b: (0, b, 0))
    return pl.pallas_call(
        pack_kernel,
        out_shape=(
            jax.ShapeDtypeStruct((blocks, 3, size, width), query_vectors.dtype),
            jax.ShapeDtypeStruct((2, tokens, width), query_vectors.dtype),
        ),
        grid=(steps,),
        in_specs=[column, column, column, row, row],
        out_specs=(
            pl.BlockSpec((blocks // steps, 3, size, width), lambda b: (b, 0, 0, 0)),
            pl.BlockSpec((2, rows, width), lambda b: (0, b, 0)),
        ),
    )(query_vectors, key_vectors, value_vectors, key_vectors, value_vectors)


def local(query_vectors, key_vectors, value_vectors):
    local_tokens = query_vectors.shape[1]
    feature_width = query_vectors.shape[2]
    heads_here = feature_width // DH
    assert local_tokens == STRIDE
    blocks = lax.axis_size("seq")
    width = STRIDE // blocks
    seq_index = lax.axis_index("seq")
    if width % 16 == 0:
        stacked, pair = pack(query_vectors, key_vectors, value_vectors, blocks)
    else:
        pair = jnp.stack([key_vectors[0], value_vectors[0]])
        stacked = jnp.stack(
            [
                query_vectors[1].reshape(blocks, width, feature_width),
                key_vectors[1].reshape(blocks, width, feature_width),
                value_vectors[1].reshape(blocks, width, feature_width),
            ],
            axis=1,
        )
    prev_pair = shifted(pair, "seq", 1)
    moved = lax.all_to_all(stacked, "seq", split_axis=0, concat_axis=0, tiled=True)
    _, prev_pair = lax.optimization_barrier((moved, prev_pair))
    grid = moved.reshape(blocks, 3, width, heads_here, DH)
    result = attend_columns(grid[:, 0], grid[:, 1], grid[:, 2])
    context = lax.all_to_all(
        result.reshape(blocks, width, feature_width), "seq", split_axis=0, concat_axis=0, tiled=True
    )
    column_out = context.reshape(local_tokens, feature_width)
    has_prev = (seq_index > 0).astype(jnp.int32).reshape(1)
    both = attend_rows(has_prev, query_vectors[0], prev_pair, key_vectors[0], value_vectors[0])
    return both.at[1].set(column_out)


def solution(mesh):
    return jax.shard_map(
        local,
        mesh=mesh,
        in_specs=(
            P(None, ("groups", "seq"), "head"),
            P(None, ("groups", "seq"), "head"),
            P(None, ("groups", "seq"), "head"),
        ),
        out_specs=P(None, ("groups", "seq"), "head"),
        check_vma=False,
    )
```

```python
import functools
import math

import jax
import jax.numpy as jnp
from jax import lax
from jax.experimental import pallas as pl
from jax.experimental.pallas import tpu as pltpu
from jax.sharding import PartitionSpec as P

DH = 128
STRIDE = 1024
QUERY_TILE = 512


def shifted(block, axis, distance):
    devices = range(lax.axis_size(axis))
    route = [(i - distance, i) for i in devices if i - distance in devices]
    return lax.ppermute(block, axis, route)


def attend_columns(query_cols, key_cols, value_cols):
    score_scale = 1.0 / math.sqrt(DH)
    scores = (
        jnp.einsum("rchd,schd->chrs", query_cols, key_cols, preferred_element_type=jnp.float32)
        * score_scale
    )
    count = query_cols.shape[0]
    row_pos = jnp.arange(count, dtype=jnp.int32)[:, None]
    other_pos = jnp.arange(count, dtype=jnp.int32)[None, :]
    allowed = other_pos <= row_pos
    scores = jnp.where(allowed[None, None], scores, -jnp.inf)
    maxima = jnp.max(scores, axis=-1, keepdims=True)
    expo = jnp.exp(scores - maxima)
    weights = (expo / jnp.sum(expo, axis=-1, keepdims=True)).astype(jnp.bfloat16)
    return jnp.einsum(
        "chrs,schd->rchd", weights, value_cols, preferred_element_type=jnp.float32
    ).astype(jnp.bfloat16)


def row_tiles(with_prev, q_ref, kp_ref, kc_ref, vp_ref, vc_ref, o_ref):
    score_scale = 1.0 / math.sqrt(DH)
    dims = (((1,), (1,)), ((), ()))
    tq = QUERY_TILE
    upper = lax.broadcasted_iota(jnp.int32, (tq, tq), 1) > lax.broadcasted_iota(
        jnp.int32, (tq, tq), 0
    )

    def scores(q, k_ref, low, high):
        return lax.dot_general(q, k_ref[low:high, :], dims, preferred_element_type=jnp.float32)

    for tile in range(STRIDE // tq):
        low, high = tile * tq, (tile + 1) * tq
        q = q_ref[low:high, :]
        parts = []
        if with_prev:
            parts.append((jnp.where(upper, scores(q, kp_ref, low, high), -jnp.inf), vp_ref, low, high))
            if high < STRIDE:
                parts.append((scores(q, kp_ref, high, STRIDE), vp_ref, high, STRIDE))
        if low > 0:
            parts.append((scores(q, kc_ref, 0, low), vc_ref, 0, low))
        parts.append((jnp.where(upper, -jnp.inf, scores(q, kc_ref, low, high)), vc_ref, low, high))
        maxima = functools.reduce(
            jnp.maximum, [jnp.max(p[0], axis=1, keepdims=True) for p in parts]
        )
        expos = [jnp.exp2((p[0] - maxima) * (score_scale * math.log2(math.e))) for p in parts]
        total = functools.reduce(jnp.add, [jnp.sum(e, axis=1, keepdims=True) for e in expos])
        inverse = 1.0 / total
        out = None
        for e, (_, v_ref, a, b) in zip(expos, parts):
            term = jnp.dot((e * inverse).astype(jnp.bfloat16), v_ref[a:b, :], preferred_element_type=jnp.float32)
            out = term if out is None else out + term
        o_ref[low:high, :] = out.astype(o_ref.dtype)


def row_kernel(flag_ref, *refs):
    has_prev = flag_ref[0] > 0

    @pl.when(has_prev)
    def _():
        row_tiles(True, *refs)

    @pl.when(jnp.logical_not(has_prev))
    def _():
        row_tiles(False, *refs)


def attend_rows(has_prev, queries, prev_pair, keys, values):
    tokens, width = queries.shape
    heads = width // DH
    spec = pl.BlockSpec((STRIDE, DH), lambda h, flag: (0, h))
    prev_key_spec = pl.BlockSpec((None, STRIDE, DH), lambda h, flag: (0, 0, h))
    prev_value_spec = pl.BlockSpec((None, STRIDE, DH), lambda h, flag: (1, 0, h))
    scores = heads * tokens * (STRIDE + QUERY_TILE)
    return pl.pallas_call(
        row_kernel,
        out_shape=jax.ShapeDtypeStruct((2, tokens, width), jnp.bfloat16),
        grid_spec=pltpu.PrefetchScalarGridSpec(
            num_scalar_prefetch=1,
            grid=(heads,),
            in_specs=[spec, prev_key_spec, spec, prev_value_spec, spec],
            out_specs=prev_key_spec,
        ),
        cost_estimate=pl.CostEstimate(
            flops=4 * scores * DH, transcendentals=scores, bytes_accessed=6 * tokens * width * 2
        ),
    )(has_prev, queries, prev_pair, keys, prev_pair, values)


def pack_kernel(q_ref, k_ref, v_ref, kp_ref, vp_ref, o_ref, pair_ref):
    shape = (o_ref.shape[0], o_ref.shape[2], o_ref.shape[3])
    o_ref[:, 0] = q_ref[...].reshape(shape)
    o_ref[:, 1] = k_ref[...].reshape(shape)
    o_ref[:, 2] = v_ref[...].reshape(shape)
    pair_ref[0] = kp_ref[...]
    pair_ref[1] = vp_ref[...]


def pack(query_vectors, key_vectors, value_vectors, blocks, steps=2):
    _, tokens, width = query_vectors.shape
    size = tokens // blocks
    rows = tokens // steps
    column = pl.BlockSpec((None, rows, width), lambda b: (1, b, 0))
    row = pl.BlockSpec((None, rows, width), lambda b: (0, b, 0))
    return pl.pallas_call(
        pack_kernel,
        out_shape=(
            jax.ShapeDtypeStruct((blocks, 3, size, width), query_vectors.dtype),
            jax.ShapeDtypeStruct((2, tokens, width), query_vectors.dtype),
        ),
        grid=(steps,),
        in_specs=[column, column, column, row, row],
        out_specs=(
            pl.BlockSpec((blocks // steps, 3, size, width), lambda b: (b, 0, 0, 0)),
            pl.BlockSpec((2, rows, width), lambda b: (0, b, 0)),
        ),
    )(query_vectors, key_vectors, value_vectors, key_vectors, value_vectors)


def local(query_vectors, key_vectors, value_vectors):
    local_tokens = query_vectors.shape[1]
    feature_width = query_vectors.shape[2]
    heads_here = feature_width // DH
    assert local_tokens == STRIDE
    blocks = lax.axis_size("seq")
    width = STRIDE // blocks
    seq_index = lax.axis_index("seq")
    if width % 16 == 0:
        stacked, pair = pack(query_vectors, key_vectors, value_vectors, blocks)
    else:
        pair = jnp.stack([key_vectors[0], value_vectors[0]])
        stacked = jnp.stack(
            [
                query_vectors[1].reshape(blocks, width, feature_width),
                key_vectors[1].reshape(blocks, width, feature_width),
                value_vectors[1].reshape(blocks, width, feature_width),
            ],
            axis=1,
        )
    prev_pair = shifted(pair, "seq", 1)
    moved = lax.all_to_all(stacked, "seq", split_axis=0, concat_axis=0, tiled=True)
    grid = moved.reshape(blocks, 3, width, heads_here, DH)
    result = attend_columns(grid[:, 0], grid[:, 1], grid[:, 2])
    result, prev_pair = lax.optimization_barrier((result, prev_pair))
    context = lax.all_to_all(
        result.reshape(blocks, width, feature_width), "seq", split_axis=0, concat_axis=0, tiled=True
    )
    column_out = context.reshape(local_tokens, feature_width)
    has_prev = (seq_index > 0).astype(jnp.int32).reshape(1)
    both = attend_rows(has_prev, query_vectors[0], prev_pair, key_vectors[0], value_vectors[0])
    return both.at[1].set(column_out)


def solution(mesh):
    return jax.shard_map(
        local,
        mesh=mesh,
        in_specs=(
            P(None, ("groups", "seq"), "head"),
            P(None, ("groups", "seq"), "head"),
            P(None, ("groups", "seq"), "head"),
        ),
        out_specs=P(None, ("groups", "seq"), "head"),
        check_vma=False,
    )
```

```python
import functools
import math

import jax
import jax.numpy as jnp
from jax import lax
from jax.experimental import pallas as pl
from jax.experimental.pallas import tpu as pltpu
from jax.sharding import PartitionSpec as P

DH = 128
STRIDE = 1024
QUERY_TILE = 512


def shifted(block, axis, distance):
    devices = range(lax.axis_size(axis))
    route = [(i - distance, i) for i in devices if i - distance in devices]
    return lax.ppermute(block, axis, route)


def attend_columns(query_cols, key_cols, value_cols):
    score_scale = 1.0 / math.sqrt(DH)
    scores = (
        jnp.einsum("rchd,schd->chrs", query_cols, key_cols, preferred_element_type=jnp.float32)
        * score_scale
    )
    count = query_cols.shape[0]
    row_pos = jnp.arange(count, dtype=jnp.int32)[:, None]
    other_pos = jnp.arange(count, dtype=jnp.int32)[None, :]
    allowed = other_pos <= row_pos
    scores = jnp.where(allowed[None, None], scores, -jnp.inf)
    maxima = jnp.max(scores, axis=-1, keepdims=True)
    expo = jnp.exp(scores - maxima)
    weights = (expo / jnp.sum(expo, axis=-1, keepdims=True)).astype(jnp.bfloat16)
    return jnp.einsum(
        "chrs,schd->rchd", weights, value_cols, preferred_element_type=jnp.float32
    ).astype(jnp.bfloat16)


def row_part(first_tile, with_prev, q_ref, kc_ref, vc_ref, prev_refs, o_ref):
    score_scale = 1.0 / math.sqrt(DH)
    dims = (((1,), (1,)), ((), ()))
    tq = QUERY_TILE
    upper = lax.broadcasted_iota(jnp.int32, (tq, tq), 1) > lax.broadcasted_iota(
        jnp.int32, (tq, tq), 0
    )

    def scores(q, k):
        return lax.dot_general(q, k, dims, preferred_element_type=jnp.float32)

    for local_tile in range(q_ref.shape[0] // tq):
        low = (first_tile + local_tile) * tq
        high = low + tq
        q = q_ref[local_tile * tq : (local_tile + 1) * tq, :]
        parts = []
        if with_prev:
            for k_ref, v_ref, start in prev_refs:
                end = start + k_ref.shape[0]
                if start <= low < end:
                    a, b = low - start, high - start
                    parts.append((jnp.where(upper, scores(q, k_ref[a:b, :]), -jnp.inf), v_ref[a:b, :]))
                    if b < end - start:
                        parts.append((scores(q, k_ref[b:, :]), v_ref[b:, :]))
                elif start >= high:
                    parts.append((scores(q, k_ref[...]), v_ref[...]))
        if low > 0:
            parts.append((scores(q, kc_ref[:low, :]), vc_ref[:low, :]))
        parts.append((jnp.where(upper, -jnp.inf, scores(q, kc_ref[low:high, :])), vc_ref[low:high, :]))
        maxima = functools.reduce(
            jnp.maximum, [jnp.max(p[0], axis=1, keepdims=True) for p in parts]
        )
        expos = [jnp.exp2((p[0] - maxima) * (score_scale * math.log2(math.e))) for p in parts]
        total = functools.reduce(jnp.add, [jnp.sum(e, axis=1, keepdims=True) for e in expos])
        inverse = 1.0 / total
        out = None
        for e, (_, v) in zip(expos, parts):
            term = jnp.dot((e * inverse).astype(jnp.bfloat16), v, preferred_element_type=jnp.float32)
            out = term if out is None else out + term
        o_ref[local_tile * tq : (local_tile + 1) * tq, :] = out.astype(o_ref.dtype)


def row_kernel(first_tile, starts, flag_ref, q_ref, kc_ref, vc_ref, *refs):
    prev_refs = [(refs[2 * i], refs[2 * i + 1], start) for i, start in enumerate(starts)]
    o_ref = refs[-1]
    has_prev = flag_ref[0] > 0

    @pl.when(has_prev)
    def _():
        row_part(first_tile, True, q_ref, kc_ref, vc_ref, prev_refs, o_ref)

    @pl.when(jnp.logical_not(has_prev))
    def _():
        row_part(first_tile, False, q_ref, kc_ref, vc_ref, prev_refs, o_ref)


def attend_rows(has_prev, half, queries, keys, values, prev_halves, buffer=None):
    tokens, width = queries.shape
    heads = width // DH
    rows = tokens // 2
    q_spec = pl.BlockSpec((rows, DH), lambda h, flag: (half, h))
    kv_spec = pl.BlockSpec((rows * (half + 1), DH), lambda h, flag: (0, h))
    key_spec = pl.BlockSpec((None, rows, DH), lambda h, flag: (0, 0, h))
    value_spec = pl.BlockSpec((None, rows, DH), lambda h, flag: (1, 0, h))
    prev_specs, prev_args, starts = [], [], []
    for start, chunk in prev_halves:
        prev_specs += [key_spec, value_spec]
        prev_args += [chunk, chunk]
        starts.append(start)
    in_specs = [q_spec, kv_spec, kv_spec] + prev_specs
    args = [has_prev, queries, keys, values] + prev_args
    aliases = {}
    if buffer is not None:
        in_specs.append(pl.BlockSpec(memory_space=pl.ANY))
        aliases = {len(args): 0}
        args.append(buffer)
    first_tile = half * (rows // QUERY_TILE)
    scores = heads * rows * (STRIDE + QUERY_TILE)
    return pl.pallas_call(
        functools.partial(row_kernel, first_tile, tuple(starts)),
        out_shape=jax.ShapeDtypeStruct((2, tokens, width), jnp.bfloat16),
        grid_spec=pltpu.PrefetchScalarGridSpec(
            num_scalar_prefetch=1,
            grid=(heads,),
            in_specs=in_specs,
            out_specs=pl.BlockSpec((None, rows, DH), lambda h, flag: (0, half, h)),
        ),
        input_output_aliases=aliases,
        cost_estimate=pl.CostEstimate(
            flops=4 * scores * DH, transcendentals=scores, bytes_accessed=4 * rows * width * 2
        ),
    )(*args)


def pack_kernel(q_ref, k_ref, v_ref, kp_ref, vp_ref, o_ref, pair_ref):
    shape = (o_ref.shape[0], o_ref.shape[2], o_ref.shape[3])
    o_ref[:, 0] = q_ref[...].reshape(shape)
    o_ref[:, 1] = k_ref[...].reshape(shape)
    o_ref[:, 2] = v_ref[...].reshape(shape)
    pair_ref[0] = kp_ref[...]
    pair_ref[1] = vp_ref[...]


def pack(query_vectors, key_vectors, value_vectors, blocks, steps=2):
    _, tokens, width = query_vectors.shape
    size = tokens // blocks
    rows = tokens // steps
    column = pl.BlockSpec((None, rows, width), lambda b: (1, b, 0))
    row = pl.BlockSpec((None, rows, width), lambda b: (0, b, 0))
    return pl.pallas_call(
        pack_kernel,
        out_shape=(
            jax.ShapeDtypeStruct((blocks, 3, size, width), query_vectors.dtype),
            jax.ShapeDtypeStruct((steps, 2, rows, width), query_vectors.dtype),
        ),
        grid=(steps,),
        in_specs=[column, column, column, row, row],
        out_specs=(
            pl.BlockSpec((blocks // steps, 3, size, width), lambda b: (b, 0, 0, 0)),
            pl.BlockSpec((None, 2, rows, width), lambda b: (b, 0, 0, 0)),
        ),
    )(query_vectors, key_vectors, value_vectors, key_vectors, value_vectors)


def local(query_vectors, key_vectors, value_vectors):
    local_tokens = query_vectors.shape[1]
    feature_width = query_vectors.shape[2]
    heads_here = feature_width // DH
    assert local_tokens == STRIDE
    blocks = lax.axis_size("seq")
    width = STRIDE // blocks
    seq_index = lax.axis_index("seq")
    half_rows = STRIDE // 2
    if width % 16 == 0:
        stacked, pair = pack(query_vectors, key_vectors, value_vectors, blocks)
    else:
        pair = jnp.stack([key_vectors[0], value_vectors[0]]).reshape(2, 2, half_rows, feature_width)
        pair = jnp.moveaxis(pair, 1, 0)
        stacked = jnp.stack(
            [
                query_vectors[1].reshape(blocks, width, feature_width),
                key_vectors[1].reshape(blocks, width, feature_width),
                value_vectors[1].reshape(blocks, width, feature_width),
            ],
            axis=1,
        )
    forward = [(i, i + 1) for i in range(blocks - 1)]
    prev_high = lax.ppermute(pair[1], "seq", forward)
    prev_low = lax.ppermute(pair[0], "seq", forward)
    moved = lax.all_to_all(stacked, "seq", split_axis=0, concat_axis=0, tiled=True)
    moved, prev_high = lax.optimization_barrier((moved, prev_high))
    grid = moved.reshape(blocks, 3, width, heads_here, DH)
    result = attend_columns(grid[:, 0], grid[:, 1], grid[:, 2])
    context = lax.all_to_all(
        result.reshape(blocks, width, feature_width), "seq", split_axis=0, concat_axis=0, tiled=True
    )
    column_out = context.reshape(local_tokens, feature_width)
    has_prev = (seq_index > 0).astype(jnp.int32).reshape(1)
    both = attend_rows(
        has_prev, 1, query_vectors[0], key_vectors[0], value_vectors[0], [(half_rows, prev_high)]
    )
    both = attend_rows(
        has_prev,
        0,
        query_vectors[0],
        key_vectors[0],
        value_vectors[0],
        [(0, prev_low), (half_rows, prev_high)],
        both,
    )
    return both.at[1].set(column_out)


def solution(mesh):
    return jax.shard_map(
        local,
        mesh=mesh,
        in_specs=(
            P(None, ("groups", "seq"), "head"),
            P(None, ("groups", "seq"), "head"),
            P(None, ("groups", "seq"), "head"),
        ),
        out_specs=P(None, ("groups", "seq"), "head"),
        check_vma=False,
    )
```

```python
import functools
import math

import jax
import jax.numpy as jnp
from jax import lax
from jax.experimental import pallas as pl
from jax.experimental.pallas import tpu as pltpu
from jax.sharding import PartitionSpec as P

DH = 128
STRIDE = 1024
QUERY_TILE = 512


def shifted(block, axis, distance):
    devices = range(lax.axis_size(axis))
    route = [(i - distance, i) for i in devices if i - distance in devices]
    return lax.ppermute(block, axis, route)


def attend_columns(query_cols, key_cols, value_cols):
    score_scale = 1.0 / math.sqrt(DH)
    scores = (
        jnp.einsum("rchd,schd->chrs", query_cols, key_cols, preferred_element_type=jnp.float32)
        * score_scale
    )
    count = query_cols.shape[0]
    row_pos = jnp.arange(count, dtype=jnp.int32)[:, None]
    other_pos = jnp.arange(count, dtype=jnp.int32)[None, :]
    allowed = other_pos <= row_pos
    scores = jnp.where(allowed[None, None], scores, -jnp.inf)
    maxima = jnp.max(scores, axis=-1, keepdims=True)
    expo = jnp.exp(scores - maxima)
    weights = (expo / jnp.sum(expo, axis=-1, keepdims=True)).astype(jnp.bfloat16)
    return jnp.einsum(
        "chrs,schd->rchd", weights, value_cols, preferred_element_type=jnp.float32
    ).astype(jnp.bfloat16)


def row_tiles(with_prev, q_ref, kp_ref, kc_ref, vp_ref, vc_ref, o_ref):
    score_scale = 1.0 / math.sqrt(DH)
    dims = (((1,), (1,)), ((), ()))
    tq = QUERY_TILE
    upper = lax.broadcasted_iota(jnp.int32, (tq, tq), 1) > lax.broadcasted_iota(
        jnp.int32, (tq, tq), 0
    )

    def scores(q, k_ref, low, high):
        return lax.dot_general(q, k_ref[low:high, :], dims, preferred_element_type=jnp.float32)

    def scores_t(q, kt_ref, low, high):
        return jnp.dot(q, kt_ref[:, low:high], preferred_element_type=jnp.float32)

    for tile in range(STRIDE // tq):
        low, high = tile * tq, (tile + 1) * tq
        q = q_ref[low:high, :]
        parts = []
        if with_prev:
            parts.append((jnp.where(upper, scores(q, kp_ref, low, high), -jnp.inf), vp_ref, low, high))
            if high < STRIDE:
                parts.append((scores(q, kp_ref, high, STRIDE), vp_ref, high, STRIDE))
        if low > 0:
            parts.append((scores_t(q, kc_ref, 0, low), vc_ref, 0, low))
        parts.append((jnp.where(upper, -jnp.inf, scores_t(q, kc_ref, low, high)), vc_ref, low, high))
        maxima = functools.reduce(
            jnp.maximum, [jnp.max(p[0], axis=1, keepdims=True) for p in parts]
        )
        expos = [jnp.exp2((p[0] - maxima) * (score_scale * math.log2(math.e))) for p in parts]
        total = functools.reduce(jnp.add, [jnp.sum(e, axis=1, keepdims=True) for e in expos])
        inverse = 1.0 / total
        out = None
        for e, (_, v_ref, a, b) in zip(expos, parts):
            term = jnp.dot((e * inverse).astype(jnp.bfloat16), v_ref[a:b, :], preferred_element_type=jnp.float32)
            out = term if out is None else out + term
        o_ref[low:high, :] = out.astype(o_ref.dtype)


def row_kernel(flag_ref, *refs):
    has_prev = flag_ref[0] > 0

    @pl.when(has_prev)
    def _():
        row_tiles(True, *refs)

    @pl.when(jnp.logical_not(has_prev))
    def _():
        row_tiles(False, *refs)


def attend_rows(has_prev, queries, prev_pair, keys, values):
    tokens, width = queries.shape
    heads = width // DH
    spec = pl.BlockSpec((STRIDE, DH), lambda h, flag: (0, h))
    prev_key_spec = pl.BlockSpec((None, STRIDE, DH), lambda h, flag: (0, 0, h))
    prev_value_spec = pl.BlockSpec((None, STRIDE, DH), lambda h, flag: (1, 0, h))
    key_t_spec = pl.BlockSpec((DH, STRIDE), lambda h, flag: (h, 0))
    scores = heads * tokens * (STRIDE + QUERY_TILE)
    return pl.pallas_call(
        row_kernel,
        out_shape=jax.ShapeDtypeStruct((2, tokens, width), jnp.bfloat16),
        grid_spec=pltpu.PrefetchScalarGridSpec(
            num_scalar_prefetch=1,
            grid=(heads,),
            in_specs=[spec, prev_key_spec, key_t_spec, prev_value_spec, spec],
            out_specs=prev_key_spec,
        ),
        cost_estimate=pl.CostEstimate(
            flops=4 * scores * DH, transcendentals=scores, bytes_accessed=6 * tokens * width * 2
        ),
    )(has_prev, queries, prev_pair, keys, prev_pair, values)


def pack_kernel(q_ref, k_ref, v_ref, kp_ref, vp_ref, o_ref, pair_ref):
    shape = (o_ref.shape[0], o_ref.shape[2], o_ref.shape[3])
    o_ref[:, 0] = q_ref[...].reshape(shape)
    o_ref[:, 1] = k_ref[...].reshape(shape)
    o_ref[:, 2] = v_ref[...].reshape(shape)
    pair_ref[0] = kp_ref[...]
    pair_ref[1] = vp_ref[...]


def pack(query_vectors, key_vectors, value_vectors, blocks, steps=2):
    _, tokens, width = query_vectors.shape
    size = tokens // blocks
    rows = tokens // steps
    column = pl.BlockSpec((None, rows, width), lambda b: (1, b, 0))
    row = pl.BlockSpec((None, rows, width), lambda b: (0, b, 0))
    return pl.pallas_call(
        pack_kernel,
        out_shape=(
            jax.ShapeDtypeStruct((blocks, 3, size, width), query_vectors.dtype),
            jax.ShapeDtypeStruct((2, tokens, width), query_vectors.dtype),
        ),
        grid=(steps,),
        in_specs=[column, column, column, row, row],
        out_specs=(
            pl.BlockSpec((blocks // steps, 3, size, width), lambda b: (b, 0, 0, 0)),
            pl.BlockSpec((2, rows, width), lambda b: (0, b, 0)),
        ),
    )(query_vectors, key_vectors, value_vectors, key_vectors, value_vectors)


def local(query_vectors, key_vectors, value_vectors):
    local_tokens = query_vectors.shape[1]
    feature_width = query_vectors.shape[2]
    heads_here = feature_width // DH
    assert local_tokens == STRIDE
    blocks = lax.axis_size("seq")
    width = STRIDE // blocks
    seq_index = lax.axis_index("seq")
    if width % 16 == 0:
        stacked, pair = pack(query_vectors, key_vectors, value_vectors, blocks)
    else:
        pair = jnp.stack([key_vectors[0], value_vectors[0]])
        stacked = jnp.stack(
            [
                query_vectors[1].reshape(blocks, width, feature_width),
                key_vectors[1].reshape(blocks, width, feature_width),
                value_vectors[1].reshape(blocks, width, feature_width),
            ],
            axis=1,
        )
    prev_pair = shifted(pair, "seq", 1)
    moved = lax.all_to_all(stacked, "seq", split_axis=0, concat_axis=0, tiled=True)
    _, prev_pair = lax.optimization_barrier((moved, prev_pair))
    grid = moved.reshape(blocks, 3, width, heads_here, DH)
    result = attend_columns(grid[:, 0], grid[:, 1], grid[:, 2])
    context = lax.all_to_all(
        result.reshape(blocks, width, feature_width), "seq", split_axis=0, concat_axis=0, tiled=True
    )
    column_out = context.reshape(local_tokens, feature_width)
    has_prev = (seq_index > 0).astype(jnp.int32).reshape(1)
    both = attend_rows(has_prev, query_vectors[0], prev_pair, key_vectors[0].T, value_vectors[0])
    return both.at[1].set(column_out)


def solution(mesh):
    return jax.shard_map(
        local,
        mesh=mesh,
        in_specs=(
            P(None, ("groups", "seq"), "head"),
            P(None, ("groups", "seq"), "head"),
            P(None, ("groups", "seq"), "head"),
        ),
        out_specs=P(None, ("groups", "seq"), "head"),
        check_vma=False,
    )
```

```python
import functools
import math

import jax
import jax.numpy as jnp
from jax import lax
from jax.experimental import pallas as pl
from jax.experimental.pallas import tpu as pltpu
from jax.sharding import PartitionSpec as P

DH = 128
STRIDE = 1024
QUERY_TILE = 256


def shifted(block, axis, distance):
    devices = range(lax.axis_size(axis))
    route = [(i - distance, i) for i in devices if i - distance in devices]
    return lax.ppermute(block, axis, route)


def attend_columns(query_cols, key_cols, value_cols):
    score_scale = 1.0 / math.sqrt(DH)
    scores = (
        jnp.einsum("rchd,schd->chrs", query_cols, key_cols, preferred_element_type=jnp.float32)
        * score_scale
    )
    count = query_cols.shape[0]
    row_pos = jnp.arange(count, dtype=jnp.int32)[:, None]
    other_pos = jnp.arange(count, dtype=jnp.int32)[None, :]
    allowed = other_pos <= row_pos
    scores = jnp.where(allowed[None, None], scores, -jnp.inf)
    maxima = jnp.max(scores, axis=-1, keepdims=True)
    expo = jnp.exp(scores - maxima)
    weights = (expo / jnp.sum(expo, axis=-1, keepdims=True)).astype(jnp.bfloat16)
    return jnp.einsum(
        "chrs,schd->rchd", weights, value_cols, preferred_element_type=jnp.float32
    ).astype(jnp.bfloat16)


def row_tiles(with_prev, q_ref, kp_ref, kc_ref, vp_ref, vc_ref, o_ref):
    score_scale = 1.0 / math.sqrt(DH)
    dims = (((1,), (1,)), ((), ()))
    tq = QUERY_TILE
    upper = lax.broadcasted_iota(jnp.int32, (tq, tq), 1) > lax.broadcasted_iota(
        jnp.int32, (tq, tq), 0
    )

    def scores(q, k_ref, low, high):
        return lax.dot_general(q, k_ref[low:high, :], dims, preferred_element_type=jnp.float32)

    def scores_t(q, kt_ref, low, high):
        return jnp.dot(q, kt_ref[:, low:high], preferred_element_type=jnp.float32)

    for tile in range(STRIDE // tq):
        low, high = tile * tq, (tile + 1) * tq
        q = q_ref[low:high, :]
        parts = []
        if with_prev:
            parts.append((jnp.where(upper, scores(q, kp_ref, low, high), -jnp.inf), vp_ref, low, high))
            if high < STRIDE:
                parts.append((scores(q, kp_ref, high, STRIDE), vp_ref, high, STRIDE))
        if low > 0:
            parts.append((scores_t(q, kc_ref, 0, low), vc_ref, 0, low))
        parts.append((jnp.where(upper, -jnp.inf, scores_t(q, kc_ref, low, high)), vc_ref, low, high))
        maxima = functools.reduce(
            jnp.maximum, [jnp.max(p[0], axis=1, keepdims=True) for p in parts]
        )
        expos = [jnp.exp2((p[0] - maxima) * (score_scale * math.log2(math.e))) for p in parts]
        total = functools.reduce(jnp.add, [jnp.sum(e, axis=1, keepdims=True) for e in expos])
        inverse = 1.0 / total
        out = None
        for e, (_, v_ref, a, b) in zip(expos, parts):
            term = jnp.dot((e * inverse).astype(jnp.bfloat16), v_ref[a:b, :], preferred_element_type=jnp.float32)
            out = term if out is None else out + term
        o_ref[low:high, :] = out.astype(o_ref.dtype)


def row_kernel(flag_ref, *refs):
    has_prev = flag_ref[0] > 0

    @pl.when(has_prev)
    def _():
        row_tiles(True, *refs)

    @pl.when(jnp.logical_not(has_prev))
    def _():
        row_tiles(False, *refs)


def attend_rows(has_prev, queries, prev_pair, keys, values):
    tokens, width = queries.shape
    heads = width // DH
    spec = pl.BlockSpec((STRIDE, DH), lambda h, flag: (0, h))
    prev_key_spec = pl.BlockSpec((None, STRIDE, DH), lambda h, flag: (0, 0, h))
    prev_value_spec = pl.BlockSpec((None, STRIDE, DH), lambda h, flag: (1, 0, h))
    key_t_spec = pl.BlockSpec((DH, STRIDE), lambda h, flag: (h, 0))
    scores = heads * tokens * (STRIDE + QUERY_TILE)
    return pl.pallas_call(
        row_kernel,
        out_shape=jax.ShapeDtypeStruct((2, tokens, width), jnp.bfloat16),
        grid_spec=pltpu.PrefetchScalarGridSpec(
            num_scalar_prefetch=1,
            grid=(heads,),
            in_specs=[spec, prev_key_spec, key_t_spec, prev_value_spec, spec],
            out_specs=prev_key_spec,
        ),
        cost_estimate=pl.CostEstimate(
            flops=4 * scores * DH, transcendentals=scores, bytes_accessed=6 * tokens * width * 2
        ),
    )(has_prev, queries, prev_pair, keys, prev_pair, values)


def pack_kernel(q_ref, k_ref, v_ref, kp_ref, vp_ref, o_ref, pair_ref):
    shape = (o_ref.shape[0], o_ref.shape[2], o_ref.shape[3])
    o_ref[:, 0] = q_ref[...].reshape(shape)
    o_ref[:, 1] = k_ref[...].reshape(shape)
    o_ref[:, 2] = v_ref[...].reshape(shape)
    pair_ref[0] = kp_ref[...]
    pair_ref[1] = vp_ref[...]


def pack(query_vectors, key_vectors, value_vectors, blocks, steps=2):
    _, tokens, width = query_vectors.shape
    size = tokens // blocks
    rows = tokens // steps
    column = pl.BlockSpec((None, rows, width), lambda b: (1, b, 0))
    row = pl.BlockSpec((None, rows, width), lambda b: (0, b, 0))
    return pl.pallas_call(
        pack_kernel,
        out_shape=(
            jax.ShapeDtypeStruct((blocks, 3, size, width), query_vectors.dtype),
            jax.ShapeDtypeStruct((2, tokens, width), query_vectors.dtype),
        ),
        grid=(steps,),
        in_specs=[column, column, column, row, row],
        out_specs=(
            pl.BlockSpec((blocks // steps, 3, size, width), lambda b: (b, 0, 0, 0)),
            pl.BlockSpec((2, rows, width), lambda b: (0, b, 0)),
        ),
    )(query_vectors, key_vectors, value_vectors, key_vectors, value_vectors)


def local(query_vectors, key_vectors, value_vectors):
    local_tokens = query_vectors.shape[1]
    feature_width = query_vectors.shape[2]
    heads_here = feature_width // DH
    assert local_tokens == STRIDE
    blocks = lax.axis_size("seq")
    width = STRIDE // blocks
    seq_index = lax.axis_index("seq")
    if width % 16 == 0:
        stacked, pair = pack(query_vectors, key_vectors, value_vectors, blocks)
    else:
        pair = jnp.stack([key_vectors[0], value_vectors[0]])
        stacked = jnp.stack(
            [
                query_vectors[1].reshape(blocks, width, feature_width),
                key_vectors[1].reshape(blocks, width, feature_width),
                value_vectors[1].reshape(blocks, width, feature_width),
            ],
            axis=1,
        )
    prev_pair = shifted(pair, "seq", 1)
    moved = lax.all_to_all(stacked, "seq", split_axis=0, concat_axis=0, tiled=True)
    _, prev_pair = lax.optimization_barrier((moved, prev_pair))
    grid = moved.reshape(blocks, 3, width, heads_here, DH)
    result = attend_columns(grid[:, 0], grid[:, 1], grid[:, 2])
    context = lax.all_to_all(
        result.reshape(blocks, width, feature_width), "seq", split_axis=0, concat_axis=0, tiled=True
    )
    column_out = context.reshape(local_tokens, feature_width)
    has_prev = (seq_index > 0).astype(jnp.int32).reshape(1)
    both = attend_rows(has_prev, query_vectors[0], prev_pair, key_vectors[0].T, value_vectors[0])
    return both.at[1].set(column_out)


def solution(mesh):
    return jax.shard_map(
        local,
        mesh=mesh,
        in_specs=(
            P(None, ("groups", "seq"), "head"),
            P(None, ("groups", "seq"), "head"),
            P(None, ("groups", "seq"), "head"),
        ),
        out_specs=P(None, ("groups", "seq"), "head"),
        check_vma=False,
    )
```

```python
import functools
import math

import jax
import jax.numpy as jnp
from jax import lax
from jax.experimental import pallas as pl
from jax.experimental.pallas import tpu as pltpu
from jax.sharding import PartitionSpec as P

DH = 128
STRIDE = 1024
QUERY_TILE = 512


def shifted(block, axis, distance):
    devices = range(lax.axis_size(axis))
    route = [(i - distance, i) for i in devices if i - distance in devices]
    return lax.ppermute(block, axis, route)


def attend_columns(query_cols, key_cols, value_cols):
    score_scale = 1.0 / math.sqrt(DH)
    scores = (
        jnp.einsum("rchd,schd->chrs", query_cols, key_cols, preferred_element_type=jnp.float32)
        * score_scale
    )
    count = query_cols.shape[0]
    row_pos = jnp.arange(count, dtype=jnp.int32)[:, None]
    other_pos = jnp.arange(count, dtype=jnp.int32)[None, :]
    allowed = other_pos <= row_pos
    scores = jnp.where(allowed[None, None], scores, -jnp.inf)
    maxima = jnp.max(scores, axis=-1, keepdims=True)
    expo = jnp.exp(scores - maxima)
    weights = (expo / jnp.sum(expo, axis=-1, keepdims=True)).astype(jnp.bfloat16)
    return jnp.einsum(
        "chrs,schd->rchd", weights, value_cols, preferred_element_type=jnp.float32
    ).astype(jnp.bfloat16)


def row_tiles(with_prev, q_ref, kp_ref, kc_ref, vp_ref, vc_ref, o_ref):
    score_scale = 1.0 / math.sqrt(DH)
    dims = (((1,), (1,)), ((), ()))
    tq = QUERY_TILE
    upper = lax.broadcasted_iota(jnp.int32, (tq, tq), 1) > lax.broadcasted_iota(
        jnp.int32, (tq, tq), 0
    )

    def scores(q, k_ref, low, high):
        return lax.dot_general(q, k_ref[low:high, :], dims, preferred_element_type=jnp.float32)

    def scores_t(q, kt_ref, low, high):
        return jnp.dot(q, kt_ref[:, low:high], preferred_element_type=jnp.float32)

    for tile in range(STRIDE // tq):
        low, high = tile * tq, (tile + 1) * tq
        q = q_ref[low:high, :]
        parts = []
        if with_prev:
            parts.append((jnp.where(upper, scores(q, kp_ref, low, high), -jnp.inf), vp_ref, low, high))
            if high < STRIDE:
                parts.append((scores(q, kp_ref, high, STRIDE), vp_ref, high, STRIDE))
        if low > 0:
            parts.append((scores_t(q, kc_ref, 0, low), vc_ref, 0, low))
        parts.append((jnp.where(upper, -jnp.inf, scores_t(q, kc_ref, low, high)), vc_ref, low, high))
        maxima = functools.reduce(
            jnp.maximum, [jnp.max(p[0], axis=1, keepdims=True) for p in parts]
        )
        expos = [jnp.exp2((p[0] - maxima) * (score_scale * math.log2(math.e))) for p in parts]
        total = functools.reduce(jnp.add, [jnp.sum(e, axis=1, keepdims=True) for e in expos])
        inverse = 1.0 / total
        out = None
        for e, (_, v_ref, a, b) in zip(expos, parts):
            term = jnp.dot((e * inverse).astype(jnp.bfloat16), v_ref[a:b, :], preferred_element_type=jnp.float32)
            out = term if out is None else out + term
        o_ref[low:high, :] = out.astype(o_ref.dtype)


def row_kernel(flag_ref, *refs):
    has_prev = flag_ref[0] > 0

    @pl.when(has_prev)
    def _():
        row_tiles(True, *refs)

    @pl.when(jnp.logical_not(has_prev))
    def _():
        row_tiles(False, *refs)


def attend_rows(has_prev, queries, prev_pair, keys, values):
    tokens, width = queries.shape
    heads = width // DH
    spec = pl.BlockSpec((STRIDE, DH), lambda h, flag: (0, h))
    prev_key_spec = pl.BlockSpec((None, STRIDE, DH), lambda h, flag: (0, 0, h))
    prev_value_spec = pl.BlockSpec((None, STRIDE, DH), lambda h, flag: (1, 0, h))
    key_t_spec = pl.BlockSpec((DH, STRIDE), lambda h, flag: (h, 0))
    scores = heads * tokens * (STRIDE + QUERY_TILE)
    return pl.pallas_call(
        row_kernel,
        out_shape=jax.ShapeDtypeStruct((2, tokens, width), jnp.bfloat16),
        grid_spec=pltpu.PrefetchScalarGridSpec(
            num_scalar_prefetch=1,
            grid=(heads,),
            in_specs=[spec, prev_key_spec, key_t_spec, prev_value_spec, spec],
            out_specs=prev_key_spec,
        ),
        cost_estimate=pl.CostEstimate(
            flops=4 * scores * DH, transcendentals=scores, bytes_accessed=6 * tokens * width * 2
        ),
    )(has_prev, queries, prev_pair, keys, prev_pair, values)


def pack_kernel(q_ref, k_ref, v_ref, kp_ref, vp_ref, o_ref, pair_ref):
    shape = (o_ref.shape[0], o_ref.shape[2], o_ref.shape[3])
    o_ref[:, 0] = q_ref[...].reshape(shape)
    o_ref[:, 1] = k_ref[...].reshape(shape)
    o_ref[:, 2] = v_ref[...].reshape(shape)
    pair_ref[0] = kp_ref[...]
    pair_ref[1] = vp_ref[...]


def pack(query_vectors, key_vectors, value_vectors, blocks, steps=1):
    _, tokens, width = query_vectors.shape
    size = tokens // blocks
    rows = tokens // steps
    column = pl.BlockSpec((None, rows, width), lambda b: (1, b, 0))
    row = pl.BlockSpec((None, rows, width), lambda b: (0, b, 0))
    return pl.pallas_call(
        pack_kernel,
        out_shape=(
            jax.ShapeDtypeStruct((blocks, 3, size, width), query_vectors.dtype),
            jax.ShapeDtypeStruct((2, tokens, width), query_vectors.dtype),
        ),
        grid=(steps,),
        in_specs=[column, column, column, row, row],
        out_specs=(
            pl.BlockSpec((blocks // steps, 3, size, width), lambda b: (b, 0, 0, 0)),
            pl.BlockSpec((2, rows, width), lambda b: (0, b, 0)),
        ),
    )(query_vectors, key_vectors, value_vectors, key_vectors, value_vectors)


def local(query_vectors, key_vectors, value_vectors):
    local_tokens = query_vectors.shape[1]
    feature_width = query_vectors.shape[2]
    heads_here = feature_width // DH
    assert local_tokens == STRIDE
    blocks = lax.axis_size("seq")
    width = STRIDE // blocks
    seq_index = lax.axis_index("seq")
    if width % 16 == 0:
        stacked, pair = pack(query_vectors, key_vectors, value_vectors, blocks)
    else:
        pair = jnp.stack([key_vectors[0], value_vectors[0]])
        stacked = jnp.stack(
            [
                query_vectors[1].reshape(blocks, width, feature_width),
                key_vectors[1].reshape(blocks, width, feature_width),
                value_vectors[1].reshape(blocks, width, feature_width),
            ],
            axis=1,
        )
    prev_pair = shifted(pair, "seq", 1)
    moved = lax.all_to_all(stacked, "seq", split_axis=0, concat_axis=0, tiled=True)
    _, prev_pair = lax.optimization_barrier((moved, prev_pair))
    grid = moved.reshape(blocks, 3, width, heads_here, DH)
    result = attend_columns(grid[:, 0], grid[:, 1], grid[:, 2])
    context = lax.all_to_all(
        result.reshape(blocks, width, feature_width), "seq", split_axis=0, concat_axis=0, tiled=True
    )
    column_out = context.reshape(local_tokens, feature_width)
    has_prev = (seq_index > 0).astype(jnp.int32).reshape(1)
    both = attend_rows(has_prev, query_vectors[0], prev_pair, key_vectors[0].T, value_vectors[0])
    return both.at[1].set(column_out)


def solution(mesh):
    return jax.shard_map(
        local,
        mesh=mesh,
        in_specs=(
            P(None, ("groups", "seq"), "head"),
            P(None, ("groups", "seq"), "head"),
            P(None, ("groups", "seq"), "head"),
        ),
        out_specs=P(None, ("groups", "seq"), "head"),
        check_vma=False,
    )
```

```python
import functools
import math

import jax
import jax.numpy as jnp
from jax import lax
from jax.experimental import pallas as pl
from jax.experimental.pallas import tpu as pltpu
from jax.sharding import PartitionSpec as P

DH = 128
STRIDE = 1024
QUERY_TILE = 512


def shifted(block, axis, distance):
    devices = range(lax.axis_size(axis))
    route = [(i - distance, i) for i in devices if i - distance in devices]
    return lax.ppermute(block, axis, route)


def attend_columns(query_cols, key_cols, value_cols):
    score_scale = 1.0 / math.sqrt(DH)
    scores = (
        jnp.einsum("rchd,schd->chrs", query_cols, key_cols, preferred_element_type=jnp.float32)
        * score_scale
    )
    count = query_cols.shape[0]
    row_pos = jnp.arange(count, dtype=jnp.int32)[:, None]
    other_pos = jnp.arange(count, dtype=jnp.int32)[None, :]
    allowed = other_pos <= row_pos
    scores = jnp.where(allowed[None, None], scores, -jnp.inf)
    maxima = jnp.max(scores, axis=-1, keepdims=True)
    expo = jnp.exp(scores - maxima)
    weights = (expo / jnp.sum(expo, axis=-1, keepdims=True)).astype(jnp.bfloat16)
    return jnp.einsum(
        "chrs,schd->rchd", weights, value_cols, preferred_element_type=jnp.float32
    ).astype(jnp.bfloat16)


def row_tiles(with_prev, q_ref, kp_ref, kc_ref, vp_ref, vc_ref, o_ref):
    score_scale = 1.0 / math.sqrt(DH)
    factor = score_scale * math.log2(math.e)
    dims = (((1,), (1,)), ((), ()))
    tq = QUERY_TILE
    half = tq // 2
    upper = lax.broadcasted_iota(jnp.int32, (half, half), 1) > lax.broadcasted_iota(
        jnp.int32, (half, half), 0
    )

    def scores(q, k_ref, low, high):
        return lax.dot_general(q, k_ref[low:high, :], dims, preferred_element_type=jnp.float32)

    def scores_t(q, kt_ref, low, high):
        return jnp.dot(q, kt_ref[:, low:high], preferred_element_type=jnp.float32)

    for tile in range(STRIDE // tq):
        low, high = tile * tq, (tile + 1) * tq
        mid = low + half
        q = q_ref[low:high, :]
        top, bottom = q[:half], q[half:]
        full, top_parts, bottom_parts = [], [], []
        if with_prev:
            top_parts.append((jnp.where(upper, scores(top, kp_ref, low, mid), -jnp.inf), vp_ref[low:mid, :]))
            top_parts.append((scores(top, kp_ref, mid, high), vp_ref[mid:high, :]))
            bottom_parts.append((jnp.where(upper, scores(bottom, kp_ref, mid, high), -jnp.inf), vp_ref[mid:high, :]))
            if high < STRIDE:
                full.append((scores(q, kp_ref, high, STRIDE), vp_ref[high:, :]))
        if low > 0:
            full.append((scores_t(q, kc_ref, 0, low), vc_ref[:low, :]))
        top_parts.append((jnp.where(upper, -jnp.inf, scores_t(top, kc_ref, low, mid)), vc_ref[low:mid, :]))
        bottom_parts.append((scores_t(bottom, kc_ref, low, mid), vc_ref[low:mid, :]))
        bottom_parts.append((jnp.where(upper, -jnp.inf, scores_t(bottom, kc_ref, mid, high)), vc_ref[mid:high, :]))

        def row_max(parts, rows):
            return [jnp.max(p[0][rows] if rows is not None else p[0], axis=1, keepdims=True) for p in parts]

        max_top = functools.reduce(
            jnp.maximum, row_max(top_parts, None) + [m[:half] for m in row_max(full, None)]
        )
        max_bottom = functools.reduce(
            jnp.maximum, row_max(bottom_parts, None) + [m[half:] for m in row_max(full, None)]
        )
        maxima = jnp.concatenate([max_top, max_bottom], axis=0)
        full_e = [jnp.exp2((p[0] - maxima) * factor) for p in full]
        top_e = [jnp.exp2((p[0] - max_top) * factor) for p in top_parts]
        bottom_e = [jnp.exp2((p[0] - max_bottom) * factor) for p in bottom_parts]
        full_sums = [jnp.sum(e, axis=1, keepdims=True) for e in full_e]
        total_top = functools.reduce(
            jnp.add, [jnp.sum(e, axis=1, keepdims=True) for e in top_e] + [t[:half] for t in full_sums]
        )
        total_bottom = functools.reduce(
            jnp.add, [jnp.sum(e, axis=1, keepdims=True) for e in bottom_e] + [t[half:] for t in full_sums]
        )
        inv_top = 1.0 / total_top
        inv_bottom = 1.0 / total_bottom
        inverse = jnp.concatenate([inv_top, inv_bottom], axis=0)

        def weighted(es, parts, inv):
            out = None
            for e, (_, v) in zip(es, parts):
                term = jnp.dot((e * inv).astype(jnp.bfloat16), v, preferred_element_type=jnp.float32)
                out = term if out is None else out + term
            return out

        out_top = weighted(top_e, top_parts, inv_top)
        out_bottom = weighted(bottom_e, bottom_parts, inv_bottom)
        out = jnp.concatenate([out_top, out_bottom], axis=0)
        if full:
            out = out + weighted(full_e, full, inverse)
        o_ref[low:high, :] = out.astype(o_ref.dtype)


def row_kernel(flag_ref, *refs):
    has_prev = flag_ref[0] > 0

    @pl.when(has_prev)
    def _():
        row_tiles(True, *refs)

    @pl.when(jnp.logical_not(has_prev))
    def _():
        row_tiles(False, *refs)


def attend_rows(has_prev, queries, prev_pair, keys, values):
    tokens, width = queries.shape
    heads = width // DH
    spec = pl.BlockSpec((STRIDE, DH), lambda h, flag: (0, h))
    prev_key_spec = pl.BlockSpec((None, STRIDE, DH), lambda h, flag: (0, 0, h))
    prev_value_spec = pl.BlockSpec((None, STRIDE, DH), lambda h, flag: (1, 0, h))
    key_t_spec = pl.BlockSpec((DH, STRIDE), lambda h, flag: (h, 0))
    scores = heads * tokens * (STRIDE + QUERY_TILE)
    return pl.pallas_call(
        row_kernel,
        out_shape=jax.ShapeDtypeStruct((2, tokens, width), jnp.bfloat16),
        grid_spec=pltpu.PrefetchScalarGridSpec(
            num_scalar_prefetch=1,
            grid=(heads,),
            in_specs=[spec, prev_key_spec, key_t_spec, prev_value_spec, spec],
            out_specs=prev_key_spec,
        ),
        cost_estimate=pl.CostEstimate(
            flops=4 * scores * DH, transcendentals=scores, bytes_accessed=6 * tokens * width * 2
        ),
    )(has_prev, queries, prev_pair, keys, prev_pair, values)


def pack_kernel(q_ref, k_ref, v_ref, kp_ref, vp_ref, o_ref, pair_ref):
    shape = (o_ref.shape[0], o_ref.shape[2], o_ref.shape[3])
    o_ref[:, 0] = q_ref[...].reshape(shape)
    o_ref[:, 1] = k_ref[...].reshape(shape)
    o_ref[:, 2] = v_ref[...].reshape(shape)
    pair_ref[0] = kp_ref[...]
    pair_ref[1] = vp_ref[...]


def pack(query_vectors, key_vectors, value_vectors, blocks, steps=2):
    _, tokens, width = query_vectors.shape
    size = tokens // blocks
    rows = tokens // steps
    column = pl.BlockSpec((None, rows, width), lambda b: (1, b, 0))
    row = pl.BlockSpec((None, rows, width), lambda b: (0, b, 0))
    return pl.pallas_call(
        pack_kernel,
        out_shape=(
            jax.ShapeDtypeStruct((blocks, 3, size, width), query_vectors.dtype),
            jax.ShapeDtypeStruct((2, tokens, width), query_vectors.dtype),
        ),
        grid=(steps,),
        in_specs=[column, column, column, row, row],
        out_specs=(
            pl.BlockSpec((blocks // steps, 3, size, width), lambda b: (b, 0, 0, 0)),
            pl.BlockSpec((2, rows, width), lambda b: (0, b, 0)),
        ),
    )(query_vectors, key_vectors, value_vectors, key_vectors, value_vectors)


def local(query_vectors, key_vectors, value_vectors):
    local_tokens = query_vectors.shape[1]
    feature_width = query_vectors.shape[2]
    heads_here = feature_width // DH
    assert local_tokens == STRIDE
    blocks = lax.axis_size("seq")
    width = STRIDE // blocks
    seq_index = lax.axis_index("seq")
    if width % 16 == 0:
        stacked, pair = pack(query_vectors, key_vectors, value_vectors, blocks)
    else:
        pair = jnp.stack([key_vectors[0], value_vectors[0]])
        stacked = jnp.stack(
            [
                query_vectors[1].reshape(blocks, width, feature_width),
                key_vectors[1].reshape(blocks, width, feature_width),
                value_vectors[1].reshape(blocks, width, feature_width),
            ],
            axis=1,
        )
    prev_pair = shifted(pair, "seq", 1)
    moved = lax.all_to_all(stacked, "seq", split_axis=0, concat_axis=0, tiled=True)
    _, prev_pair = lax.optimization_barrier((moved, prev_pair))
    grid = moved.reshape(blocks, 3, width, heads_here, DH)
    result = attend_columns(grid[:, 0], grid[:, 1], grid[:, 2])
    context = lax.all_to_all(
        result.reshape(blocks, width, feature_width), "seq", split_axis=0, concat_axis=0, tiled=True
    )
    column_out = context.reshape(local_tokens, feature_width)
    has_prev = (seq_index > 0).astype(jnp.int32).reshape(1)
    both = attend_rows(has_prev, query_vectors[0], prev_pair, key_vectors[0].T, value_vectors[0])
    return both.at[1].set(column_out)


def solution(mesh):
    return jax.shard_map(
        local,
        mesh=mesh,
        in_specs=(
            P(None, ("groups", "seq"), "head"),
            P(None, ("groups", "seq"), "head"),
            P(None, ("groups", "seq"), "head"),
        ),
        out_specs=P(None, ("groups", "seq"), "head"),
        check_vma=False,
    )
```

```python
import functools
import math

import jax
import jax.numpy as jnp
from jax import lax
from jax.experimental import pallas as pl
from jax.experimental.pallas import tpu as pltpu
from jax.sharding import PartitionSpec as P

DH = 128
STRIDE = 1024
QUERY_TILE = 1024


def shifted(block, axis, distance):
    devices = range(lax.axis_size(axis))
    route = [(i - distance, i) for i in devices if i - distance in devices]
    return lax.ppermute(block, axis, route)


def attend_columns(query_cols, key_cols, value_cols):
    score_scale = 1.0 / math.sqrt(DH)
    scores = (
        jnp.einsum("rchd,schd->chrs", query_cols, key_cols, preferred_element_type=jnp.float32)
        * score_scale
    )
    count = query_cols.shape[0]
    row_pos = jnp.arange(count, dtype=jnp.int32)[:, None]
    other_pos = jnp.arange(count, dtype=jnp.int32)[None, :]
    allowed = other_pos <= row_pos
    scores = jnp.where(allowed[None, None], scores, -jnp.inf)
    maxima = jnp.max(scores, axis=-1, keepdims=True)
    expo = jnp.exp(scores - maxima)
    weights = (expo / jnp.sum(expo, axis=-1, keepdims=True)).astype(jnp.bfloat16)
    return jnp.einsum(
        "chrs,schd->rchd", weights, value_cols, preferred_element_type=jnp.float32
    ).astype(jnp.bfloat16)


def row_tiles(with_prev, q_ref, kp_ref, kc_ref, vp_ref, vc_ref, o_ref):
    score_scale = 1.0 / math.sqrt(DH)
    dims = (((1,), (1,)), ((), ()))
    tq = QUERY_TILE
    upper = lax.broadcasted_iota(jnp.int32, (tq, tq), 1) > lax.broadcasted_iota(
        jnp.int32, (tq, tq), 0
    )

    def scores(q, k_ref, low, high):
        return lax.dot_general(q, k_ref[low:high, :], dims, preferred_element_type=jnp.float32)

    def scores_t(q, kt_ref, low, high):
        return jnp.dot(q, kt_ref[:, low:high], preferred_element_type=jnp.float32)

    for tile in range(STRIDE // tq):
        low, high = tile * tq, (tile + 1) * tq
        q = q_ref[low:high, :]
        parts = []
        if with_prev:
            parts.append((jnp.where(upper, scores(q, kp_ref, low, high), -jnp.inf), vp_ref, low, high))
            if high < STRIDE:
                parts.append((scores(q, kp_ref, high, STRIDE), vp_ref, high, STRIDE))
        if low > 0:
            parts.append((scores_t(q, kc_ref, 0, low), vc_ref, 0, low))
        parts.append((jnp.where(upper, -jnp.inf, scores_t(q, kc_ref, low, high)), vc_ref, low, high))
        maxima = functools.reduce(
            jnp.maximum, [jnp.max(p[0], axis=1, keepdims=True) for p in parts]
        )
        expos = [jnp.exp2((p[0] - maxima) * (score_scale * math.log2(math.e))) for p in parts]
        total = functools.reduce(jnp.add, [jnp.sum(e, axis=1, keepdims=True) for e in expos])
        inverse = 1.0 / total
        out = None
        for e, (_, v_ref, a, b) in zip(expos, parts):
            term = jnp.dot((e * inverse).astype(jnp.bfloat16), v_ref[a:b, :], preferred_element_type=jnp.float32)
            out = term if out is None else out + term
        o_ref[low:high, :] = out.astype(o_ref.dtype)


def row_kernel(flag_ref, *refs):
    has_prev = flag_ref[0] > 0

    @pl.when(has_prev)
    def _():
        row_tiles(True, *refs)

    @pl.when(jnp.logical_not(has_prev))
    def _():
        row_tiles(False, *refs)


def attend_rows(has_prev, queries, prev_pair, keys, values):
    tokens, width = queries.shape
    heads = width // DH
    spec = pl.BlockSpec((STRIDE, DH), lambda h, flag: (0, h))
    prev_key_spec = pl.BlockSpec((None, STRIDE, DH), lambda h, flag: (0, 0, h))
    prev_value_spec = pl.BlockSpec((None, STRIDE, DH), lambda h, flag: (1, 0, h))
    key_t_spec = pl.BlockSpec((DH, STRIDE), lambda h, flag: (h, 0))
    scores = heads * tokens * (STRIDE + QUERY_TILE)
    return pl.pallas_call(
        row_kernel,
        out_shape=jax.ShapeDtypeStruct((2, tokens, width), jnp.bfloat16),
        grid_spec=pltpu.PrefetchScalarGridSpec(
            num_scalar_prefetch=1,
            grid=(heads,),
            in_specs=[spec, prev_key_spec, key_t_spec, prev_value_spec, spec],
            out_specs=prev_key_spec,
        ),
        cost_estimate=pl.CostEstimate(
            flops=4 * scores * DH, transcendentals=scores, bytes_accessed=6 * tokens * width * 2
        ),
    )(has_prev, queries, prev_pair, keys, prev_pair, values)


def pack_kernel(q_ref, k_ref, v_ref, kp_ref, vp_ref, o_ref, pair_ref):
    shape = (o_ref.shape[0], o_ref.shape[2], o_ref.shape[3])
    o_ref[:, 0] = q_ref[...].reshape(shape)
    o_ref[:, 1] = k_ref[...].reshape(shape)
    o_ref[:, 2] = v_ref[...].reshape(shape)
    pair_ref[0] = kp_ref[...]
    pair_ref[1] = vp_ref[...]


def pack(query_vectors, key_vectors, value_vectors, blocks, steps=2):
    _, tokens, width = query_vectors.shape
    size = tokens // blocks
    rows = tokens // steps
    column = pl.BlockSpec((None, rows, width), lambda b: (1, b, 0))
    row = pl.BlockSpec((None, rows, width), lambda b: (0, b, 0))
    return pl.pallas_call(
        pack_kernel,
        out_shape=(
            jax.ShapeDtypeStruct((blocks, 3, size, width), query_vectors.dtype),
            jax.ShapeDtypeStruct((2, tokens, width), query_vectors.dtype),
        ),
        grid=(steps,),
        in_specs=[column, column, column, row, row],
        out_specs=(
            pl.BlockSpec((blocks // steps, 3, size, width), lambda b: (b, 0, 0, 0)),
            pl.BlockSpec((2, rows, width), lambda b: (0, b, 0)),
        ),
    )(query_vectors, key_vectors, value_vectors, key_vectors, value_vectors)


def local(query_vectors, key_vectors, value_vectors):
    local_tokens = query_vectors.shape[1]
    feature_width = query_vectors.shape[2]
    heads_here = feature_width // DH
    assert local_tokens == STRIDE
    blocks = lax.axis_size("seq")
    width = STRIDE // blocks
    seq_index = lax.axis_index("seq")
    if width % 16 == 0:
        stacked, pair = pack(query_vectors, key_vectors, value_vectors, blocks)
    else:
        pair = jnp.stack([key_vectors[0], value_vectors[0]])
        stacked = jnp.stack(
            [
                query_vectors[1].reshape(blocks, width, feature_width),
                key_vectors[1].reshape(blocks, width, feature_width),
                value_vectors[1].reshape(blocks, width, feature_width),
            ],
            axis=1,
        )
    prev_pair = shifted(pair, "seq", 1)
    moved = lax.all_to_all(stacked, "seq", split_axis=0, concat_axis=0, tiled=True)
    _, prev_pair = lax.optimization_barrier((moved, prev_pair))
    grid = moved.reshape(blocks, 3, width, heads_here, DH)
    result = attend_columns(grid[:, 0], grid[:, 1], grid[:, 2])
    context = lax.all_to_all(
        result.reshape(blocks, width, feature_width), "seq", split_axis=0, concat_axis=0, tiled=True
    )
    column_out = context.reshape(local_tokens, feature_width)
    has_prev = (seq_index > 0).astype(jnp.int32).reshape(1)
    both = attend_rows(has_prev, query_vectors[0], prev_pair, key_vectors[0].T, value_vectors[0])
    return both.at[1].set(column_out)


def solution(mesh):
    return jax.shard_map(
        local,
        mesh=mesh,
        in_specs=(
            P(None, ("groups", "seq"), "head"),
            P(None, ("groups", "seq"), "head"),
            P(None, ("groups", "seq"), "head"),
        ),
        out_specs=P(None, ("groups", "seq"), "head"),
        check_vma=False,
    )
```

```python
import functools
import math

import jax
import jax.numpy as jnp
from jax import lax
from jax.experimental import pallas as pl
from jax.experimental.pallas import tpu as pltpu
from jax.sharding import PartitionSpec as P

DH = 128
STRIDE = 1024
QUERY_TILE = 512


def shifted(block, axis, distance):
    devices = range(lax.axis_size(axis))
    route = [(i - distance, i) for i in devices if i - distance in devices]
    return lax.ppermute(block, axis, route)


def attend_columns(query_cols, key_cols, value_cols):
    score_scale = 1.0 / math.sqrt(DH)
    scores = (
        jnp.einsum("rchd,schd->chrs", query_cols, key_cols, preferred_element_type=jnp.float32)
        * score_scale
    )
    count = query_cols.shape[0]
    row_pos = jnp.arange(count, dtype=jnp.int32)[:, None]
    other_pos = jnp.arange(count, dtype=jnp.int32)[None, :]
    allowed = other_pos <= row_pos
    scores = jnp.where(allowed[None, None], scores, -jnp.inf)
    maxima = jnp.max(scores, axis=-1, keepdims=True)
    expo = jnp.exp(scores - maxima)
    weights = (expo / jnp.sum(expo, axis=-1, keepdims=True)).astype(jnp.bfloat16)
    return jnp.einsum(
        "chrs,schd->rchd", weights, value_cols, preferred_element_type=jnp.float32
    ).astype(jnp.bfloat16)


def row_tiles(with_prev, q_ref, kp_ref, kc_ref, vp_ref, vc_ref, o_ref):
    score_scale = 1.0 / math.sqrt(DH)
    dims = (((1,), (1,)), ((), ()))
    tq = QUERY_TILE

    for tile in range(STRIDE // tq):
        low, high = tile * tq, (tile + 1) * tq
        q = q_ref[low:high, :]
        parts = []
        if with_prev:
            s = lax.dot_general(q, kp_ref[low:, :], dims, preferred_element_type=jnp.float32)
            shape = (tq, STRIDE - low)
            ok = lax.broadcasted_iota(jnp.int32, shape, 1) > lax.broadcasted_iota(jnp.int32, shape, 0)
            parts.append((jnp.where(ok, s, -jnp.inf), vp_ref[low:, :]))
        s = jnp.dot(q, kc_ref[:, :high], preferred_element_type=jnp.float32)
        shape = (tq, high)
        ok = lax.broadcasted_iota(jnp.int32, shape, 1) <= lax.broadcasted_iota(jnp.int32, shape, 0) + low
        parts.append((jnp.where(ok, s, -jnp.inf), vc_ref[:high, :]))
        maxima = functools.reduce(
            jnp.maximum, [jnp.max(p[0], axis=1, keepdims=True) for p in parts]
        )
        expos = [jnp.exp2((p[0] - maxima) * (score_scale * math.log2(math.e))) for p in parts]
        total = functools.reduce(jnp.add, [jnp.sum(e, axis=1, keepdims=True) for e in expos])
        inverse = 1.0 / total
        out = None
        for e, (_, v) in zip(expos, parts):
            term = jnp.dot((e * inverse).astype(jnp.bfloat16), v, preferred_element_type=jnp.float32)
            out = term if out is None else out + term
        o_ref[low:high, :] = out.astype(o_ref.dtype)


def row_kernel(flag_ref, *refs):
    has_prev = flag_ref[0] > 0

    @pl.when(has_prev)
    def _():
        row_tiles(True, *refs)

    @pl.when(jnp.logical_not(has_prev))
    def _():
        row_tiles(False, *refs)


def attend_rows(has_prev, queries, prev_pair, keys, values):
    tokens, width = queries.shape
    heads = width // DH
    spec = pl.BlockSpec((STRIDE, DH), lambda h, flag: (0, h))
    prev_key_spec = pl.BlockSpec((None, STRIDE, DH), lambda h, flag: (0, 0, h))
    prev_value_spec = pl.BlockSpec((None, STRIDE, DH), lambda h, flag: (1, 0, h))
    key_t_spec = pl.BlockSpec((DH, STRIDE), lambda h, flag: (h, 0))
    scores = heads * tokens * (STRIDE + QUERY_TILE)
    return pl.pallas_call(
        row_kernel,
        out_shape=jax.ShapeDtypeStruct((2, tokens, width), jnp.bfloat16),
        grid_spec=pltpu.PrefetchScalarGridSpec(
            num_scalar_prefetch=1,
            grid=(heads,),
            in_specs=[spec, prev_key_spec, key_t_spec, prev_value_spec, spec],
            out_specs=prev_key_spec,
        ),
        cost_estimate=pl.CostEstimate(
            flops=4 * scores * DH, transcendentals=scores, bytes_accessed=6 * tokens * width * 2
        ),
    )(has_prev, queries, prev_pair, keys, prev_pair, values)


def pack_kernel(q_ref, k_ref, v_ref, kp_ref, vp_ref, o_ref, pair_ref):
    shape = (o_ref.shape[0], o_ref.shape[2], o_ref.shape[3])
    o_ref[:, 0] = q_ref[...].reshape(shape)
    o_ref[:, 1] = k_ref[...].reshape(shape)
    o_ref[:, 2] = v_ref[...].reshape(shape)
    pair_ref[0] = kp_ref[...]
    pair_ref[1] = vp_ref[...]


def pack(query_vectors, key_vectors, value_vectors, blocks, steps=2):
    _, tokens, width = query_vectors.shape
    size = tokens // blocks
    rows = tokens // steps
    column = pl.BlockSpec((None, rows, width), lambda b: (1, b, 0))
    row = pl.BlockSpec((None, rows, width), lambda b: (0, b, 0))
    return pl.pallas_call(
        pack_kernel,
        out_shape=(
            jax.ShapeDtypeStruct((blocks, 3, size, width), query_vectors.dtype),
            jax.ShapeDtypeStruct((2, tokens, width), query_vectors.dtype),
        ),
        grid=(steps,),
        in_specs=[column, column, column, row, row],
        out_specs=(
            pl.BlockSpec((blocks // steps, 3, size, width), lambda b: (b, 0, 0, 0)),
            pl.BlockSpec((2, rows, width), lambda b: (0, b, 0)),
        ),
    )(query_vectors, key_vectors, value_vectors, key_vectors, value_vectors)


def local(query_vectors, key_vectors, value_vectors):
    local_tokens = query_vectors.shape[1]
    feature_width = query_vectors.shape[2]
    heads_here = feature_width // DH
    assert local_tokens == STRIDE
    blocks = lax.axis_size("seq")
    width = STRIDE // blocks
    seq_index = lax.axis_index("seq")
    if width % 16 == 0:
        stacked, pair = pack(query_vectors, key_vectors, value_vectors, blocks)
    else:
        pair = jnp.stack([key_vectors[0], value_vectors[0]])
        stacked = jnp.stack(
            [
                query_vectors[1].reshape(blocks, width, feature_width),
                key_vectors[1].reshape(blocks, width, feature_width),
                value_vectors[1].reshape(blocks, width, feature_width),
            ],
            axis=1,
        )
    prev_pair = shifted(pair, "seq", 1)
    moved = lax.all_to_all(stacked, "seq", split_axis=0, concat_axis=0, tiled=True)
    _, prev_pair = lax.optimization_barrier((moved, prev_pair))
    grid = moved.reshape(blocks, 3, width, heads_here, DH)
    result = attend_columns(grid[:, 0], grid[:, 1], grid[:, 2])
    context = lax.all_to_all(
        result.reshape(blocks, width, feature_width), "seq", split_axis=0, concat_axis=0, tiled=True
    )
    column_out = context.reshape(local_tokens, feature_width)
    has_prev = (seq_index > 0).astype(jnp.int32).reshape(1)
    both = attend_rows(has_prev, query_vectors[0], prev_pair, key_vectors[0].T, value_vectors[0])
    return both.at[1].set(column_out)


def solution(mesh):
    return jax.shard_map(
        local,
        mesh=mesh,
        in_specs=(
            P(None, ("groups", "seq"), "head"),
            P(None, ("groups", "seq"), "head"),
            P(None, ("groups", "seq"), "head"),
        ),
        out_specs=P(None, ("groups", "seq"), "head"),
        check_vma=False,
    )
```

```python
import functools
import math

import jax
import jax.numpy as jnp
from jax import lax
from jax.experimental import pallas as pl
from jax.experimental.pallas import tpu as pltpu
from jax.sharding import PartitionSpec as P

DH = 128
STRIDE = 1024
QUERY_TILE = 512


def shifted(block, axis, distance):
    devices = range(lax.axis_size(axis))
    route = [(i - distance, i) for i in devices if i - distance in devices]
    return lax.ppermute(block, axis, route)


def attend_columns(query_cols, key_cols, value_cols):
    score_scale = 1.0 / math.sqrt(DH)
    queries = query_cols.astype(jnp.float32)
    keys = key_cols.astype(jnp.float32)
    scores = jnp.sum(queries[:, None] * keys[None, :], axis=-1) * score_scale
    count = query_cols.shape[0]
    row_pos = jnp.arange(count, dtype=jnp.int32)[:, None, None, None]
    other_pos = jnp.arange(count, dtype=jnp.int32)[None, :, None, None]
    scores = jnp.where(other_pos <= row_pos, scores, -jnp.inf)
    maxima = jnp.max(scores, axis=1, keepdims=True)
    expo = jnp.exp(scores - maxima)
    weights = (expo / jnp.sum(expo, axis=1, keepdims=True)).astype(jnp.bfloat16)
    out = jnp.sum(
        weights.astype(jnp.float32)[..., None] * value_cols.astype(jnp.float32)[None], axis=1
    )
    return out.astype(jnp.bfloat16)


def row_tiles(with_prev, q_ref, kp_ref, kc_ref, vp_ref, vc_ref, o_ref):
    score_scale = 1.0 / math.sqrt(DH)
    dims = (((1,), (1,)), ((), ()))
    tq = QUERY_TILE
    upper = lax.broadcasted_iota(jnp.int32, (tq, tq), 1) > lax.broadcasted_iota(
        jnp.int32, (tq, tq), 0
    )

    def scores(q, k_ref, low, high):
        return lax.dot_general(q, k_ref[low:high, :], dims, preferred_element_type=jnp.float32)

    def scores_t(q, kt_ref, low, high):
        return jnp.dot(q, kt_ref[:, low:high], preferred_element_type=jnp.float32)

    for tile in range(STRIDE // tq):
        low, high = tile * tq, (tile + 1) * tq
        q = q_ref[low:high, :]
        parts = []
        if with_prev:
            parts.append((jnp.where(upper, scores(q, kp_ref, low, high), -jnp.inf), vp_ref, low, high))
            if high < STRIDE:
                parts.append((scores(q, kp_ref, high, STRIDE), vp_ref, high, STRIDE))
        if low > 0:
            parts.append((scores_t(q, kc_ref, 0, low), vc_ref, 0, low))
        parts.append((jnp.where(upper, -jnp.inf, scores_t(q, kc_ref, low, high)), vc_ref, low, high))
        maxima = functools.reduce(
            jnp.maximum, [jnp.max(p[0], axis=1, keepdims=True) for p in parts]
        )
        expos = [jnp.exp2((p[0] - maxima) * (score_scale * math.log2(math.e))) for p in parts]
        total = functools.reduce(jnp.add, [jnp.sum(e, axis=1, keepdims=True) for e in expos])
        inverse = 1.0 / total
        out = None
        for e, (_, v_ref, a, b) in zip(expos, parts):
            term = jnp.dot((e * inverse).astype(jnp.bfloat16), v_ref[a:b, :], preferred_element_type=jnp.float32)
            out = term if out is None else out + term
        o_ref[low:high, :] = out.astype(o_ref.dtype)


def row_kernel(flag_ref, *refs):
    has_prev = flag_ref[0] > 0

    @pl.when(has_prev)
    def _():
        row_tiles(True, *refs)

    @pl.when(jnp.logical_not(has_prev))
    def _():
        row_tiles(False, *refs)


def attend_rows(has_prev, queries, prev_pair, keys, values):
    tokens, width = queries.shape
    heads = width // DH
    spec = pl.BlockSpec((STRIDE, DH), lambda h, flag: (0, h))
    prev_key_spec = pl.BlockSpec((None, STRIDE, DH), lambda h, flag: (0, 0, h))
    prev_value_spec = pl.BlockSpec((None, STRIDE, DH), lambda h, flag: (1, 0, h))
    key_t_spec = pl.BlockSpec((DH, STRIDE), lambda h, flag: (h, 0))
    scores = heads * tokens * (STRIDE + QUERY_TILE)
    return pl.pallas_call(
        row_kernel,
        out_shape=jax.ShapeDtypeStruct((2, tokens, width), jnp.bfloat16),
        grid_spec=pltpu.PrefetchScalarGridSpec(
            num_scalar_prefetch=1,
            grid=(heads,),
            in_specs=[spec, prev_key_spec, key_t_spec, prev_value_spec, spec],
            out_specs=prev_key_spec,
        ),
        cost_estimate=pl.CostEstimate(
            flops=4 * scores * DH, transcendentals=scores, bytes_accessed=6 * tokens * width * 2
        ),
    )(has_prev, queries, prev_pair, keys, prev_pair, values)


def pack_kernel(q_ref, k_ref, v_ref, kp_ref, vp_ref, o_ref, pair_ref):
    shape = (o_ref.shape[0], o_ref.shape[2], o_ref.shape[3])
    o_ref[:, 0] = q_ref[...].reshape(shape)
    o_ref[:, 1] = k_ref[...].reshape(shape)
    o_ref[:, 2] = v_ref[...].reshape(shape)
    pair_ref[0] = kp_ref[...]
    pair_ref[1] = vp_ref[...]


def pack(query_vectors, key_vectors, value_vectors, blocks, steps=2):
    _, tokens, width = query_vectors.shape
    size = tokens // blocks
    rows = tokens // steps
    column = pl.BlockSpec((None, rows, width), lambda b: (1, b, 0))
    row = pl.BlockSpec((None, rows, width), lambda b: (0, b, 0))
    return pl.pallas_call(
        pack_kernel,
        out_shape=(
            jax.ShapeDtypeStruct((blocks, 3, size, width), query_vectors.dtype),
            jax.ShapeDtypeStruct((2, tokens, width), query_vectors.dtype),
        ),
        grid=(steps,),
        in_specs=[column, column, column, row, row],
        out_specs=(
            pl.BlockSpec((blocks // steps, 3, size, width), lambda b: (b, 0, 0, 0)),
            pl.BlockSpec((2, rows, width), lambda b: (0, b, 0)),
        ),
    )(query_vectors, key_vectors, value_vectors, key_vectors, value_vectors)


def local(query_vectors, key_vectors, value_vectors):
    local_tokens = query_vectors.shape[1]
    feature_width = query_vectors.shape[2]
    heads_here = feature_width // DH
    assert local_tokens == STRIDE
    blocks = lax.axis_size("seq")
    width = STRIDE // blocks
    seq_index = lax.axis_index("seq")
    if width % 16 == 0:
        stacked, pair = pack(query_vectors, key_vectors, value_vectors, blocks)
    else:
        pair = jnp.stack([key_vectors[0], value_vectors[0]])
        stacked = jnp.stack(
            [
                query_vectors[1].reshape(blocks, width, feature_width),
                key_vectors[1].reshape(blocks, width, feature_width),
                value_vectors[1].reshape(blocks, width, feature_width),
            ],
            axis=1,
        )
    prev_pair = shifted(pair, "seq", 1)
    moved = lax.all_to_all(stacked, "seq", split_axis=0, concat_axis=0, tiled=True)
    _, prev_pair = lax.optimization_barrier((moved, prev_pair))
    grid = moved.reshape(blocks, 3, width, heads_here, DH)
    result = attend_columns(grid[:, 0], grid[:, 1], grid[:, 2])
    context = lax.all_to_all(
        result.reshape(blocks, width, feature_width), "seq", split_axis=0, concat_axis=0, tiled=True
    )
    column_out = context.reshape(local_tokens, feature_width)
    has_prev = (seq_index > 0).astype(jnp.int32).reshape(1)
    both = attend_rows(has_prev, query_vectors[0], prev_pair, key_vectors[0].T, value_vectors[0])
    return both.at[1].set(column_out)


def solution(mesh):
    return jax.shard_map(
        local,
        mesh=mesh,
        in_specs=(
            P(None, ("groups", "seq"), "head"),
            P(None, ("groups", "seq"), "head"),
            P(None, ("groups", "seq"), "head"),
        ),
        out_specs=P(None, ("groups", "seq"), "head"),
        check_vma=False,
    )
```

```python
import functools
import math

import jax
import jax.numpy as jnp
from jax import lax
from jax.experimental import pallas as pl
from jax.experimental.pallas import tpu as pltpu
from jax.sharding import PartitionSpec as P

DH = 128
STRIDE = 1024
QUERY_TILE = 256


def shifted(block, axis, distance):
    devices = range(lax.axis_size(axis))
    route = [(i - distance, i) for i in devices if i - distance in devices]
    return lax.ppermute(block, axis, route)


def attend_columns(query_cols, key_cols, value_cols):
    score_scale = 1.0 / math.sqrt(DH)
    scores = (
        jnp.einsum("rchd,schd->chrs", query_cols, key_cols, preferred_element_type=jnp.float32)
        * score_scale
    )
    count = query_cols.shape[0]
    row_pos = jnp.arange(count, dtype=jnp.int32)[:, None]
    other_pos = jnp.arange(count, dtype=jnp.int32)[None, :]
    allowed = other_pos <= row_pos
    scores = jnp.where(allowed[None, None], scores, -jnp.inf)
    maxima = jnp.max(scores, axis=-1, keepdims=True)
    expo = jnp.exp(scores - maxima)
    weights = (expo / jnp.sum(expo, axis=-1, keepdims=True)).astype(jnp.bfloat16)
    return jnp.einsum(
        "chrs,schd->rchd", weights, value_cols, preferred_element_type=jnp.float32
    ).astype(jnp.bfloat16)


def row_tiles(with_prev, q_ref, kp_ref, kc_ref, vp_ref, vc_ref, o_ref):
    score_scale = 1.0 / math.sqrt(DH)
    dims = (((1,), (1,)), ((), ()))
    tq = QUERY_TILE

    for tile in range(STRIDE // tq):
        low, high = tile * tq, (tile + 1) * tq
        q = q_ref[low:high, :]
        parts = []
        if with_prev:
            s = lax.dot_general(q, kp_ref[low:, :], dims, preferred_element_type=jnp.float32)
            shape = (tq, STRIDE - low)
            ok = lax.broadcasted_iota(jnp.int32, shape, 1) > lax.broadcasted_iota(jnp.int32, shape, 0)
            parts.append((jnp.where(ok, s, -jnp.inf), vp_ref[low:, :]))
        s = jnp.dot(q, kc_ref[:, :high], preferred_element_type=jnp.float32)
        shape = (tq, high)
        ok = lax.broadcasted_iota(jnp.int32, shape, 1) <= lax.broadcasted_iota(jnp.int32, shape, 0) + low
        parts.append((jnp.where(ok, s, -jnp.inf), vc_ref[:high, :]))
        maxima = functools.reduce(
            jnp.maximum, [jnp.max(p[0], axis=1, keepdims=True) for p in parts]
        )
        expos = [jnp.exp2((p[0] - maxima) * (score_scale * math.log2(math.e))) for p in parts]
        total = functools.reduce(jnp.add, [jnp.sum(e, axis=1, keepdims=True) for e in expos])
        inverse = 1.0 / total
        out = None
        for e, (_, v) in zip(expos, parts):
            term = jnp.dot((e * inverse).astype(jnp.bfloat16), v, preferred_element_type=jnp.float32)
            out = term if out is None else out + term
        o_ref[low:high, :] = out.astype(o_ref.dtype)


def row_kernel(flag_ref, *refs):
    has_prev = flag_ref[0] > 0

    @pl.when(has_prev)
    def _():
        row_tiles(True, *refs)

    @pl.when(jnp.logical_not(has_prev))
    def _():
        row_tiles(False, *refs)


def attend_rows(has_prev, queries, prev_pair, keys, values):
    tokens, width = queries.shape
    heads = width // DH
    spec = pl.BlockSpec((STRIDE, DH), lambda h, flag: (0, h))
    prev_key_spec = pl.BlockSpec((None, STRIDE, DH), lambda h, flag: (0, 0, h))
    prev_value_spec = pl.BlockSpec((None, STRIDE, DH), lambda h, flag: (1, 0, h))
    key_t_spec = pl.BlockSpec((DH, STRIDE), lambda h, flag: (h, 0))
    scores = heads * tokens * (STRIDE + QUERY_TILE)
    return pl.pallas_call(
        row_kernel,
        out_shape=jax.ShapeDtypeStruct((2, tokens, width), jnp.bfloat16),
        grid_spec=pltpu.PrefetchScalarGridSpec(
            num_scalar_prefetch=1,
            grid=(heads,),
            in_specs=[spec, prev_key_spec, key_t_spec, prev_value_spec, spec],
            out_specs=prev_key_spec,
        ),
        cost_estimate=pl.CostEstimate(
            flops=4 * scores * DH, transcendentals=scores, bytes_accessed=6 * tokens * width * 2
        ),
    )(has_prev, queries, prev_pair, keys, prev_pair, values)


def pack_kernel(q_ref, k_ref, v_ref, kp_ref, vp_ref, o_ref, pair_ref):
    shape = (o_ref.shape[0], o_ref.shape[2], o_ref.shape[3])
    o_ref[:, 0] = q_ref[...].reshape(shape)
    o_ref[:, 1] = k_ref[...].reshape(shape)
    o_ref[:, 2] = v_ref[...].reshape(shape)
    pair_ref[0] = kp_ref[...]
    pair_ref[1] = vp_ref[...]


def pack(query_vectors, key_vectors, value_vectors, blocks, steps=2):
    _, tokens, width = query_vectors.shape
    size = tokens // blocks
    rows = tokens // steps
    column = pl.BlockSpec((None, rows, width), lambda b: (1, b, 0))
    row = pl.BlockSpec((None, rows, width), lambda b: (0, b, 0))
    return pl.pallas_call(
        pack_kernel,
        out_shape=(
            jax.ShapeDtypeStruct((blocks, 3, size, width), query_vectors.dtype),
            jax.ShapeDtypeStruct((2, tokens, width), query_vectors.dtype),
        ),
        grid=(steps,),
        in_specs=[column, column, column, row, row],
        out_specs=(
            pl.BlockSpec((blocks // steps, 3, size, width), lambda b: (b, 0, 0, 0)),
            pl.BlockSpec((2, rows, width), lambda b: (0, b, 0)),
        ),
    )(query_vectors, key_vectors, value_vectors, key_vectors, value_vectors)


def local(query_vectors, key_vectors, value_vectors):
    local_tokens = query_vectors.shape[1]
    feature_width = query_vectors.shape[2]
    heads_here = feature_width // DH
    assert local_tokens == STRIDE
    blocks = lax.axis_size("seq")
    width = STRIDE // blocks
    seq_index = lax.axis_index("seq")
    if width % 16 == 0:
        stacked, pair = pack(query_vectors, key_vectors, value_vectors, blocks)
    else:
        pair = jnp.stack([key_vectors[0], value_vectors[0]])
        stacked = jnp.stack(
            [
                query_vectors[1].reshape(blocks, width, feature_width),
                key_vectors[1].reshape(blocks, width, feature_width),
                value_vectors[1].reshape(blocks, width, feature_width),
            ],
            axis=1,
        )
    prev_pair = shifted(pair, "seq", 1)
    moved = lax.all_to_all(stacked, "seq", split_axis=0, concat_axis=0, tiled=True)
    _, prev_pair = lax.optimization_barrier((moved, prev_pair))
    grid = moved.reshape(blocks, 3, width, heads_here, DH)
    result = attend_columns(grid[:, 0], grid[:, 1], grid[:, 2])
    context = lax.all_to_all(
        result.reshape(blocks, width, feature_width), "seq", split_axis=0, concat_axis=0, tiled=True
    )
    column_out = context.reshape(local_tokens, feature_width)
    has_prev = (seq_index > 0).astype(jnp.int32).reshape(1)
    both = attend_rows(has_prev, query_vectors[0], prev_pair, key_vectors[0].T, value_vectors[0])
    return both.at[1].set(column_out)


def solution(mesh):
    return jax.shard_map(
        local,
        mesh=mesh,
        in_specs=(
            P(None, ("groups", "seq"), "head"),
            P(None, ("groups", "seq"), "head"),
            P(None, ("groups", "seq"), "head"),
        ),
        out_specs=P(None, ("groups", "seq"), "head"),
        check_vma=False,
    )
```

```python
import functools
import math

import jax
import jax.numpy as jnp
from jax import lax
from jax.experimental import pallas as pl
from jax.experimental.pallas import tpu as pltpu
from jax.sharding import PartitionSpec as P

DH = 128
STRIDE = 1024
QUERY_TILE = 512


def shifted(block, axis, distance):
    devices = range(lax.axis_size(axis))
    route = [(i - distance, i) for i in devices if i - distance in devices]
    return lax.ppermute(block, axis, route)


def attend_columns(query_cols, key_cols, value_cols):
    score_scale = 1.0 / math.sqrt(DH)
    scores = (
        jnp.einsum("rchd,schd->chrs", query_cols, key_cols, preferred_element_type=jnp.float32)
        * score_scale
    )
    count = query_cols.shape[0]
    row_pos = jnp.arange(count, dtype=jnp.int32)[:, None]
    other_pos = jnp.arange(count, dtype=jnp.int32)[None, :]
    allowed = other_pos <= row_pos
    scores = jnp.where(allowed[None, None], scores, -jnp.inf)
    maxima = jnp.max(scores, axis=-1, keepdims=True)
    expo = jnp.exp(scores - maxima)
    weights = (expo / jnp.sum(expo, axis=-1, keepdims=True)).astype(jnp.bfloat16)
    return jnp.einsum(
        "chrs,schd->rchd", weights, value_cols, preferred_element_type=jnp.float32
    ).astype(jnp.bfloat16)


def row_tiles(with_prev, q_ref, kp_ref, kc_ref, vp_ref, vc_ref, o_ref):
    score_scale = 1.0 / math.sqrt(DH)
    dims = (((1,), (1,)), ((), ()))
    tq = QUERY_TILE
    upper = lax.broadcasted_iota(jnp.int32, (tq, tq), 1) > lax.broadcasted_iota(
        jnp.int32, (tq, tq), 0
    )

    def scores(q, k_ref, low, high):
        return lax.dot_general(q, k_ref[low:high, :], dims, preferred_element_type=jnp.float32)

    def scores_t(q, kt_ref, low, high):
        return jnp.dot(q, kt_ref[:, low:high], preferred_element_type=jnp.float32)

    for tile in range(STRIDE // tq):
        low, high = tile * tq, (tile + 1) * tq
        q = q_ref[low:high, :]
        parts = []
        if with_prev:
            parts.append((jnp.where(upper, scores(q, kp_ref, low, high), -jnp.inf), vp_ref, low, high))
            if high < STRIDE:
                parts.append((scores(q, kp_ref, high, STRIDE), vp_ref, high, STRIDE))
        if low > 0:
            parts.append((scores_t(q, kc_ref, 0, low), vc_ref, 0, low))
        parts.append((jnp.where(upper, -jnp.inf, scores_t(q, kc_ref, low, high)), vc_ref, low, high))
        maxima = functools.reduce(
            jnp.maximum, [jnp.max(p[0], axis=1, keepdims=True) for p in parts]
        )
        expos = [jnp.exp2((p[0] - maxima) * (score_scale * math.log2(math.e))) for p in parts]
        total = functools.reduce(jnp.add, [jnp.sum(e, axis=1, keepdims=True) for e in expos])
        inverse = 1.0 / total
        out = None
        for e, (_, v_ref, a, b) in zip(expos, parts):
            term = jnp.dot((e * inverse).astype(jnp.bfloat16), v_ref[a:b, :], preferred_element_type=jnp.float32)
            out = term if out is None else out + term
        o_ref[low:high, :] = out.astype(o_ref.dtype)


def row_kernel(flag_ref, *refs):
    has_prev = flag_ref[0] > 0

    @pl.when(has_prev)
    def _():
        row_tiles(True, *refs)

    @pl.when(jnp.logical_not(has_prev))
    def _():
        row_tiles(False, *refs)


def attend_rows(has_prev, queries, prev_pair, keys, values):
    tokens, width = queries.shape
    heads = width // DH
    spec = pl.BlockSpec((STRIDE, DH), lambda h, flag: (0, h))
    prev_key_spec = pl.BlockSpec((None, STRIDE, DH), lambda h, flag: (0, 0, h))
    prev_value_spec = pl.BlockSpec((None, STRIDE, DH), lambda h, flag: (1, 0, h))
    key_t_spec = pl.BlockSpec((DH, STRIDE), lambda h, flag: (h, 0))
    scores = heads * tokens * (STRIDE + QUERY_TILE)
    return pl.pallas_call(
        row_kernel,
        out_shape=jax.ShapeDtypeStruct((2, tokens, width), jnp.bfloat16),
        grid_spec=pltpu.PrefetchScalarGridSpec(
            num_scalar_prefetch=1,
            grid=(heads,),
            in_specs=[spec, prev_key_spec, key_t_spec, prev_value_spec, spec],
            out_specs=prev_key_spec,
        ),
        cost_estimate=pl.CostEstimate(
            flops=4 * scores * DH, transcendentals=scores, bytes_accessed=6 * tokens * width * 2
        ),
    )(has_prev, queries, prev_pair, keys, prev_pair, values)


def pack_kernel(q_ref, k_ref, v_ref, kp_ref, vp_ref, o_ref, pair_ref):
    shape = (o_ref.shape[0], o_ref.shape[2], o_ref.shape[3])
    o_ref[:, 0] = q_ref[...].reshape(shape)
    o_ref[:, 1] = k_ref[...].reshape(shape)
    o_ref[:, 2] = v_ref[...].reshape(shape)
    pair_ref[0] = kp_ref[...]
    pair_ref[1] = vp_ref[...]


def pack(query_vectors, key_vectors, value_vectors, blocks, steps=4):
    _, tokens, width = query_vectors.shape
    size = tokens // blocks
    rows = tokens // steps
    column = pl.BlockSpec((None, rows, width), lambda b: (1, b, 0))
    row = pl.BlockSpec((None, rows, width), lambda b: (0, b, 0))
    return pl.pallas_call(
        pack_kernel,
        out_shape=(
            jax.ShapeDtypeStruct((blocks, 3, size, width), query_vectors.dtype),
            jax.ShapeDtypeStruct((2, tokens, width), query_vectors.dtype),
        ),
        grid=(steps,),
        in_specs=[column, column, column, row, row],
        out_specs=(
            pl.BlockSpec((blocks // steps, 3, size, width), lambda b: (b, 0, 0, 0)),
            pl.BlockSpec((2, rows, width), lambda b: (0, b, 0)),
        ),
    )(query_vectors, key_vectors, value_vectors, key_vectors, value_vectors)


def local(query_vectors, key_vectors, value_vectors):
    local_tokens = query_vectors.shape[1]
    feature_width = query_vectors.shape[2]
    heads_here = feature_width // DH
    assert local_tokens == STRIDE
    blocks = lax.axis_size("seq")
    width = STRIDE // blocks
    seq_index = lax.axis_index("seq")
    if width % 16 == 0:
        stacked, pair = pack(query_vectors, key_vectors, value_vectors, blocks)
    else:
        pair = jnp.stack([key_vectors[0], value_vectors[0]])
        stacked = jnp.stack(
            [
                query_vectors[1].reshape(blocks, width, feature_width),
                key_vectors[1].reshape(blocks, width, feature_width),
                value_vectors[1].reshape(blocks, width, feature_width),
            ],
            axis=1,
        )
    prev_pair = shifted(pair, "seq", 1)
    moved = lax.all_to_all(stacked, "seq", split_axis=0, concat_axis=0, tiled=True)
    _, prev_pair = lax.optimization_barrier((moved, prev_pair))
    grid = moved.reshape(blocks, 3, width, heads_here, DH)
    result = attend_columns(grid[:, 0], grid[:, 1], grid[:, 2])
    context = lax.all_to_all(
        result.reshape(blocks, width, feature_width), "seq", split_axis=0, concat_axis=0, tiled=True
    )
    column_out = context.reshape(local_tokens, feature_width)
    has_prev = (seq_index > 0).astype(jnp.int32).reshape(1)
    both = attend_rows(has_prev, query_vectors[0], prev_pair, key_vectors[0].T, value_vectors[0])
    return both.at[1].set(column_out)


def solution(mesh):
    return jax.shard_map(
        local,
        mesh=mesh,
        in_specs=(
            P(None, ("groups", "seq"), "head"),
            P(None, ("groups", "seq"), "head"),
            P(None, ("groups", "seq"), "head"),
        ),
        out_specs=P(None, ("groups", "seq"), "head"),
        check_vma=False,
    )
```

```python
import functools
import math

import jax
import jax.numpy as jnp
from jax import lax
from jax.experimental import pallas as pl
from jax.experimental.pallas import tpu as pltpu
from jax.sharding import PartitionSpec as P

DH = 128
STRIDE = 1024
QUERY_TILE = 512


def shifted(block, axis, distance):
    devices = range(lax.axis_size(axis))
    route = [(i - distance, i) for i in devices if i - distance in devices]
    return lax.ppermute(block, axis, route)


def attend_columns(query_cols, key_cols, value_cols):
    score_scale = 1.0 / math.sqrt(DH)
    scores = (
        jnp.einsum("rchd,schd->chrs", query_cols, key_cols, preferred_element_type=jnp.float32)
        * score_scale
    )
    count = query_cols.shape[0]
    row_pos = jnp.arange(count, dtype=jnp.int32)[:, None]
    other_pos = jnp.arange(count, dtype=jnp.int32)[None, :]
    allowed = other_pos <= row_pos
    scores = jnp.where(allowed[None, None], scores, -jnp.inf)
    maxima = jnp.max(scores, axis=-1, keepdims=True)
    expo = jnp.exp(scores - maxima)
    weights = (expo / jnp.sum(expo, axis=-1, keepdims=True)).astype(jnp.bfloat16)
    return jnp.einsum(
        "chrs,schd->rchd", weights, value_cols, preferred_element_type=jnp.float32
    ).astype(jnp.bfloat16)


def row_tiles(with_prev, q_ref, kp_ref, kc_ref, vp_ref, vc_ref, o_ref):
    score_scale = 1.0 / math.sqrt(DH)
    dims = (((1,), (1,)), ((), ()))
    tq = QUERY_TILE
    upper = lax.broadcasted_iota(jnp.int32, (tq, tq), 1) > lax.broadcasted_iota(
        jnp.int32, (tq, tq), 0
    )

    def scores(q, k_ref, low, high):
        return lax.dot_general(q, k_ref[low:high, :], dims, preferred_element_type=jnp.float32)

    def scores_t(q, kt_ref, low, high):
        return jnp.dot(q, kt_ref[:, low:high], preferred_element_type=jnp.float32)

    for tile in range(STRIDE // tq):
        low, high = tile * tq, (tile + 1) * tq
        q = q_ref[low:high, :]
        parts = []
        if with_prev:
            parts.append((jnp.where(upper, scores(q, kp_ref, low, high), -jnp.inf), vp_ref, low, high))
            if high < STRIDE:
                parts.append((scores(q, kp_ref, high, STRIDE), vp_ref, high, STRIDE))
        if low > 0:
            parts.append((scores_t(q, kc_ref, 0, low), vc_ref, 0, low))
        parts.append((jnp.where(upper, -jnp.inf, scores_t(q, kc_ref, low, high)), vc_ref, low, high))
        maxima = functools.reduce(
            jnp.maximum, [jnp.max(p[0], axis=1, keepdims=True) for p in parts]
        )
        expos = [jnp.exp2((p[0] - maxima) * (score_scale * math.log2(math.e))) for p in parts]
        total = functools.reduce(jnp.add, [jnp.sum(e, axis=1, keepdims=True) for e in expos])
        inverse = 1.0 / total
        out = None
        for e, (_, v_ref, a, b) in zip(expos, parts):
            term = jnp.dot((e * inverse).astype(jnp.bfloat16), v_ref[a:b, :], preferred_element_type=jnp.float32)
            out = term if out is None else out + term
        o_ref[low:high, :] = out.astype(o_ref.dtype)


def row_kernel(flag_ref, *refs):
    has_prev = flag_ref[0] > 0

    @pl.when(has_prev)
    def _():
        row_tiles(True, *refs)

    @pl.when(jnp.logical_not(has_prev))
    def _():
        row_tiles(False, *refs)


def attend_rows(has_prev, queries, prev_pair, keys, values):
    tokens, width = queries.shape
    heads = width // DH
    spec = pl.BlockSpec((STRIDE, DH), lambda h, flag: (0, h))
    prev_key_spec = pl.BlockSpec((None, STRIDE, DH), lambda h, flag: (0, 0, h))
    prev_value_spec = pl.BlockSpec((None, STRIDE, DH), lambda h, flag: (1, 0, h))
    key_t_spec = pl.BlockSpec((DH, STRIDE), lambda h, flag: (h, 0))
    scores = heads * tokens * (STRIDE + QUERY_TILE)
    return pl.pallas_call(
        row_kernel,
        out_shape=jax.ShapeDtypeStruct((2, tokens, width), jnp.bfloat16),
        grid_spec=pltpu.PrefetchScalarGridSpec(
            num_scalar_prefetch=1,
            grid=(heads,),
            in_specs=[spec, prev_key_spec, key_t_spec, prev_value_spec, spec],
            out_specs=prev_key_spec,
        ),
        cost_estimate=pl.CostEstimate(
            flops=4 * scores * DH, transcendentals=scores, bytes_accessed=6 * tokens * width * 2
        ),
    )(has_prev, queries, prev_pair, keys, prev_pair, values)


def pack_kernel(q_ref, k_ref, v_ref, kp_ref, vp_ref, o_ref, pair_ref):
    shape = (o_ref.shape[0], o_ref.shape[2], o_ref.shape[3])
    o_ref[:, 0] = q_ref[...].reshape(shape)
    o_ref[:, 1] = k_ref[...].reshape(shape)
    o_ref[:, 2] = v_ref[...].reshape(shape)
    pair_ref[0] = kp_ref[...]
    pair_ref[1] = vp_ref[...]


def pack(query_vectors, key_vectors, value_vectors, blocks, steps=2):
    _, tokens, width = query_vectors.shape
    size = tokens // blocks
    rows = tokens // steps
    column = pl.BlockSpec((None, rows, width), lambda b: (1, b, 0))
    row = pl.BlockSpec((None, rows, width), lambda b: (0, b, 0))
    return pl.pallas_call(
        pack_kernel,
        out_shape=(
            jax.ShapeDtypeStruct((blocks, 3, size, width), query_vectors.dtype),
            jax.ShapeDtypeStruct((2, tokens, width), query_vectors.dtype),
        ),
        grid=(steps,),
        in_specs=[column, column, column, row, row],
        out_specs=(
            pl.BlockSpec((blocks // steps, 3, size, width), lambda b: (b, 0, 0, 0)),
            pl.BlockSpec((2, rows, width), lambda b: (0, b, 0)),
        ),
    )(query_vectors, key_vectors, value_vectors, key_vectors, value_vectors)


def local(query_vectors, key_vectors, value_vectors):
    local_tokens = query_vectors.shape[1]
    feature_width = query_vectors.shape[2]
    heads_here = feature_width // DH
    assert local_tokens == STRIDE
    blocks = lax.axis_size("seq")
    width = STRIDE // blocks
    seq_index = lax.axis_index("seq")
    if width % 16 == 0:
        stacked, pair = pack(query_vectors, key_vectors, value_vectors, blocks)
    else:
        pair = jnp.stack([key_vectors[0], value_vectors[0]])
        stacked = jnp.stack(
            [
                query_vectors[1].reshape(blocks, width, feature_width),
                key_vectors[1].reshape(blocks, width, feature_width),
                value_vectors[1].reshape(blocks, width, feature_width),
            ],
            axis=1,
        )
    prev_pair = shifted(pair, "seq", 1)
    moved = lax.all_to_all(stacked, "seq", split_axis=0, concat_axis=0, tiled=True)
    _, prev_pair = lax.optimization_barrier((moved, prev_pair))
    grid = moved.reshape(blocks, 3, width, heads_here, DH)
    result = attend_columns(grid[:, 0], grid[:, 1], grid[:, 2])
    context = lax.all_to_all(result, "seq", split_axis=0, concat_axis=0, tiled=True)
    column_out = context.reshape(local_tokens, feature_width)
    has_prev = (seq_index > 0).astype(jnp.int32).reshape(1)
    both = attend_rows(has_prev, query_vectors[0], prev_pair, key_vectors[0].T, value_vectors[0])
    return both.at[1].set(column_out)


def solution(mesh):
    return jax.shard_map(
        local,
        mesh=mesh,
        in_specs=(
            P(None, ("groups", "seq"), "head"),
            P(None, ("groups", "seq"), "head"),
            P(None, ("groups", "seq"), "head"),
        ),
        out_specs=P(None, ("groups", "seq"), "head"),
        check_vma=False,
    )
```
